32 devices in a mesh: lat: 4 (over x, core), lon: 2 (over y), lev: 4 (over z).
Axes of the slice: x: 2, y: 2, z: 4, core: 2. Of those that a mesh axis runs over, the one named last changes fastest.
Arguments:
- fields: float32 [2, 60, 128, 256], P(None, 'lev', 'lat', 'lon'), may hold values from -6 to 6
- diffusivity: float32 [60, 128, 256], P('lev', 'lat', 'lon'), may hold values from 0.02 to 0.24
- cloudy_index: int32 [4, 2048], P('lat', 'lon'), may hold values from 0 to 4095, as said below
- owners: int32 [4, 2048, 1], P('lat', 'lon'), may hold values from 0 to 1; in each aligned block of 256 rows (0 to 255, 256 to 511, ..., all dimensions but the last counted through in order) at most 256 rows name the same one
- w_in: bfloat16 [2, 120, 1024], P('lon'), may hold values from -0.5 to 0.5
- w_mid: bfloat16 [2, 2, 1024, 1024], P('lon'), may hold values from -0.1875 to 0.1875
- w_out: bfloat16 [2, 1024, 120], P('lon'), may hold values from -0.1875 to 0.1875
Outputs:
- fields_next: float32 [2, 60, 128, 256], P(None, 'lev', 'lat', 'lon')
The draws below stay inside these ranges and needn't reach their ends.
Inputs may be any that keep to these rules, and one draw needn't show every extreme that they name: `cloudy_index`: in row i, entries j * 1024 to (j + 1) * 1024 - 1 are distinct column numbers a * 128 + b of the dycore block (i, j). `owners`: in each aligned block of 256 rows (one level slice of one dycore block), no regime is named by more than 256 rows.
All inputs are finite; a program needn't handle non-finite values.
Results may differ from the reference program's by a relative error of at most 0.00062.
Values may be sent and summed in bfloat16 or wider, within the bound.
No kernel may reach another device: no remote copies, remote signals or barrier semaphores. Data moves between devices by JAX's collectives and lax.ppermute only.
A program may use at most 64 MiB of HBM per device.

```python
import math
import jax
import jax.numpy as jnp
import numpy as np
from jax import lax

LEVELS = 60
HID = 1024
STEPS = 3
LAT_DEV = 32
LON_DEV = 128
SUB = 256
CLOUDY = 1024
CAP = 256
FEAT = 120
GRID_LAT = 128
GRID_LON = 256
N_LAT = 4
N_LON = 2


def draw_cloudy_index(key, part):
    cells = LAT_DEV * LON_DEV
    subkeys = jax.random.split(key, N_LAT * N_LON + 1)
    chosen = jax.vmap(lambda subkey: jax.random.permutation(subkey, cells)[:CLOUDY])(subkeys[1:])
    inner = jax.random.permutation(subkeys[0], cells - 2)[:CLOUDY - 2] + 1
    leading = jnp.concatenate([jnp.array([cells - 1, 0], jnp.int32), inner.astype(jnp.int32)])
    chosen = chosen.at[0].set(leading.astype(chosen.dtype))
    return chosen.reshape(N_LAT, N_LON * CLOUDY).astype(jnp.int32)


def steps_of(rng, shape, pieces, smallest, top_value):
    def one(axis_at, blocks):
        heights = jax.random.uniform(jax.random.fold_in(jax.random.fold_in(rng, 6), axis_at), (blocks,), jnp.float32, smallest / len(pieces), top_value / len(pieces))
        return jnp.repeat(jnp.exp(heights), shape[axis_at] // blocks).reshape((-1,) + (1,) * (len(shape) - axis_at - 1))

    level = one(*pieces[0])
    for cut in pieces[1:]:
        level = level * one(*cut)
    return level


def routed_block(rng, own, number, rows, amount, top, limit, lean):
    order = jax.random.permutation(rng, amount)
    heavy_load, common = shares(amount, rows * top, limit, lean, True), shares(amount, rows * top, limit, lean, False)
    places = jnp.arange(amount)

    def named(lengths, offset_by):
        used = int((lengths > 0).sum())
        fixed = max(1, used // 4)
        passed = fixed + (places - fixed + offset_by * (used - fixed)) % max(1, amount - fixed)
        return jnp.zeros((amount,), jnp.int32).at[order[jnp.where(places < fixed, places, passed)]].set(jnp.asarray(lengths, jnp.int32))

    lengths = jnp.where(number % 4 == 0, named(heavy_load, number // 4), named(common, number - number // 4 - 1))
    mixed = jax.random.permutation(jax.random.fold_in(own, 3), amount)
    donor, sink = mixed[0:amount // 2 * 2:2], mixed[1:amount // 2 * 2:2]
    margin = jnp.minimum(lengths[donor] - 1, limit - lengths[sink]) // 2
    margin = jnp.where((donor == order[0]) | (sink == order[0]) | (lengths[sink] == 0), 0, jnp.maximum(margin, 0))
    passed = jax.random.randint(jax.random.fold_in(own, 4), (amount // 2,), 0, 1 << 20) % (margin + 1)
    lengths = lengths.at[donor].add(-passed).at[sink].add(passed)
    items = jnp.searchsorted(jnp.cumsum(lengths), jnp.arange(rows * top), side="right").astype(jnp.int32)
    grid = items.reshape(top, rows).T
    grid = grid[jax.random.permutation(jax.random.fold_in(own, 1), rows)]
    offset_by = jax.random.randint(jax.random.fold_in(own, 2), (rows, 1), 0, top)
    return jnp.take_along_axis(grid, (jnp.arange(top)[None, :] + offset_by) % top, axis=1)


def shares(amount, total, limit, slope, full):
    weights = [(1 << 20) // math.isqrt(rank ** slope) + 1 for rank in range(1, amount + 1)]
    largest = limit if full else min(limit, max(-(-total // amount), total * weights[0] // sum(weights)))
    least = 1 if total - largest >= amount - 1 else 0
    given, spare = [largest] + [least] * (amount - 1), total - largest - least * (amount - 1)
    while spare > 0:
        free = [i for i in range(1, amount) if given[i] < largest] or [i for i in range(1, amount) if given[i] < limit]
        mass, left = sum([weights[i] for i in free]), spare
        for i in free:
            more = min(limit - given[i], max(1, left * weights[i] // mass), spare)
            given[i] = given[i] + more
            spare = spare - more
    return np.array(given)


def gaussian(rng, dims, width, most, cuts=(), kind=jnp.bfloat16):
    entries = width * jax.random.normal(rng, dims, jnp.float32)
    if cuts:
        entries = entries * steps_of(rng, dims, cuts, -0.22, 0.18)
    return jnp.clip(entries, -most, most).astype(kind)


def setup_inputs(seed: int = 0) -> dict:
    streams_of = jax.random.split(jax.random.key(seed), 8)
    fields = gaussian(streams_of[0], (2, LEVELS, GRID_LAT, GRID_LON), 1.0, 6.0, ((1, 4), (2, 4), (3, 2)), jnp.float32)
    diffusivity = jnp.clip(jnp.exp(math.log(0.24) - 2.4849066 * jax.random.uniform(streams_of[1], (LEVELS, GRID_LAT, GRID_LON), jnp.float32) ** steps_of(streams_of[1], (LEVELS, GRID_LAT, GRID_LON), ((0, 4), (1, 4), (2, 2)), -0.2, 0.2)), 0.02, 0.24)
    cloudy_index = draw_cloudy_index(jax.random.fold_in(streams_of[7], 71), 0)
    owners_keys = jax.random.split(jax.random.fold_in(streams_of[3], 1), N_LAT * (N_LON * CLOUDY) // SUB)
    owners_turns = jax.random.permutation(jax.random.fold_in(streams_of[3], 3), N_LAT * (N_LON * CLOUDY) // SUB)
    owners = jax.vmap(lambda own, number: routed_block(jax.random.fold_in(streams_of[3], 2), own, number, SUB, N_LON, 1, CAP, 2))(owners_keys, owners_turns).reshape((N_LAT, N_LON * CLOUDY, 1))
    w_in = gaussian(streams_of[4], (N_LON, FEAT, HID), FEAT ** -0.5, 0.5, ((0, 2),))
    w_mid = gaussian(streams_of[5], (N_LON, 2, HID, HID), HID ** -0.5, 0.1875, ((0, 2),))
    w_out = gaussian(streams_of[6], (N_LON, HID, FEAT), HID ** -0.5, 0.1875, ((0, 2),))
    return dict(fields=fields, diffusivity=diffusivity, cloudy_index=cloudy_index, owners=owners, w_in=w_in, w_mid=w_mid, w_out=w_out)


def pad_grid(values):
    padded = jnp.pad(values, [(0, 0)] * (values.ndim - 2) + [(1, 1), (0, 0)])
    return jnp.concatenate([padded[..., -1:], padded, padded[..., :1]], axis=-1)


def substep(values, coefficients):
    centre = values[..., 1:-1, 1:-1]
    middle = coefficients[:, 1:-1, 1:-1]
    updated = centre
    for lat_cut, lon_cut in ((slice(0, -2), slice(1, -1)), (slice(2, None), slice(1, -1)), (slice(1, -1), slice(0, -2)), (slice(1, -1), slice(2, None))):
        neighbour = values[..., lat_cut, lon_cut]
        face_coef = 0.5 * (middle + coefficients[:, lat_cut, lon_cut])
        updated = updated + face_coef * (neighbour - centre)
    return updated


def network(block_rows, w_first, w_middle, w_last):
    hidden = jax.nn.gelu(jnp.dot(block_rows, w_first, preferred_element_type=jnp.float32)).astype(jnp.bfloat16)
    for layer_no in range(w_middle.shape[0]):
        hidden = jax.nn.gelu(jnp.dot(hidden, w_middle[layer_no], preferred_element_type=jnp.float32)).astype(jnp.bfloat16)
    return jnp.dot(hidden, w_last, preferred_element_type=jnp.float32).astype(jnp.bfloat16)


def reference(fields, diffusivity, cloudy_index, owners, w_in, w_mid, w_out):
    padded_kappa = pad_grid(diffusivity)
    values = fields
    for repeat in range(STEPS):
        values = substep(pad_grid(values), padded_kappa)
    column_ids = cloudy_index.reshape(N_LAT, N_LON, CLOUDY).astype(jnp.int32)
    lat_base = (jnp.arange(N_LAT).astype(jnp.int32) * LAT_DEV)[:, None, None]
    lon_base = (jnp.arange(N_LON).astype(jnp.int32) * LON_DEV)[None, :, None]
    row_lat = (lat_base + column_ids // LON_DEV).reshape(-1).astype(jnp.int32)
    row_lon = (lon_base + column_ids % LON_DEV).reshape(-1).astype(jnp.int32)
    routes = owners.reshape(-1).astype(jnp.int32)
    count_all = row_lat.shape[0]
    columns = values[:, :, row_lat, row_lon].astype(jnp.bfloat16).reshape(FEAT, count_all).T
    group_rows = 512
    onehot = (routes[:, None] == jnp.arange(N_LON).astype(jnp.int32)[None, :]).astype(jnp.int32)
    slot_rank = (jnp.sum(jnp.cumsum(onehot, 0) * onehot, 1) - 1).astype(jnp.int32)
    counts = jnp.sum(onehot, 0).astype(jnp.int32)
    padded_counts = ((counts + group_rows - 1) // group_rows * group_rows).astype(jnp.int32)
    starts = (jnp.cumsum(padded_counts) - padded_counts).astype(jnp.int32)
    target = (starts[routes] + slot_rank).astype(jnp.int32)
    groups = -(-count_all // group_rows) + N_LON
    slot_table = jnp.full((groups * group_rows,), count_all, jnp.int32).at[target].set(jnp.arange(count_all).astype(jnp.int32))
    group_start = (jnp.arange(groups).astype(jnp.int32) * group_rows)[:, None]
    group_expert = (jnp.sum((group_start >= starts[None, :]).astype(jnp.int32), 1) - 1).astype(jnp.int32)
    padded_rows = jnp.concatenate([columns, jnp.zeros((1, FEAT), jnp.bfloat16)], 0)

    def one_group(inputs):
        row_ids, expert = inputs
        return network(padded_rows[row_ids], w_in[expert], w_mid[expert], w_out[expert])

    outcome = lax.map(one_group, (slot_table.reshape(groups, group_rows), group_expert))
    result = jnp.zeros((count_all + 1, FEAT), jnp.bfloat16).at[slot_table].set(outcome.reshape(-1, FEAT))
    tendency = result[:count_all].T.reshape(2, LEVELS, count_all).astype(jnp.float32)
    return values.at[:, :, row_lat, row_lon].add(tendency)
```

```python
import jax
import jax.numpy as jnp
from jax import lax
from jax.sharding import PartitionSpec as P

LEVELS = 60
STEPS = 3


def halo_exchange(cells, width):
    lat_count = lax.axis_size("lat")
    from_above = lax.ppermute(
        cells[..., cells.shape[-2] - width :, :], "lat", [(i, i + 1) for i in range(lat_count - 1)]
    )
    from_below = lax.ppermute(
        cells[..., :width, :], "lat", [(i + 1, i) for i in range(lat_count - 1)]
    )
    cells = jnp.concatenate([from_above, cells, from_below], axis=-2)
    lon_count = lax.axis_size("lon")
    left = cells[..., :width]
    right = cells[..., cells.shape[-1] - width :]
    if lon_count == 2:
        both = lax.ppermute(jnp.concatenate([right, left], axis=-1), "lon", [(0, 1), (1, 0)])
        from_left, from_right = both[..., :width], both[..., width:]
    else:
        from_left = lax.ppermute(right, "lon", [(i, (i + 1) % lon_count) for i in range(lon_count)])
        from_right = lax.ppermute(left, "lon", [((i + 1) % lon_count, i) for i in range(lon_count)])
    return jnp.concatenate([from_left, cells, from_right], axis=-1)


def substep(values, coefficients):
    centre = values[..., 1:-1, 1:-1]
    middle = coefficients[:, 1:-1, 1:-1]
    updated = centre
    for lat_cut, lon_cut in (
        (slice(0, -2), slice(1, -1)),
        (slice(2, None), slice(1, -1)),
        (slice(1, -1), slice(0, -2)),
        (slice(1, -1), slice(2, None)),
    ):
        neighbour = values[..., lat_cut, lon_cut]
        face_coef = 0.5 * (middle + coefficients[:, lat_cut, lon_cut])
        updated = updated + face_coef * (neighbour - centre)
    return updated


def clear_outside(values, rim_width, lat_rows):
    lat_pos = (
        lax.axis_index("lat") * lat_rows - rim_width + jnp.arange(values.shape[-2], dtype=jnp.int32)
    )
    inside = (lat_pos >= 0) & (lat_pos < lat_rows * lax.axis_size("lat"))
    return jnp.where(inside[:, None], values, 0.0)


def dynamics(fields, diffusivity):
    kinds, level_rows, lat_rows, lon_cols = fields.shape
    stacked = jnp.concatenate(
        [fields.reshape(kinds * level_rows, lat_rows, lon_cols), diffusivity], axis=0
    )
    stacked = halo_exchange(stacked, STEPS)
    values = stacked[: kinds * level_rows].reshape(
        kinds, level_rows, lat_rows + 2 * STEPS, lon_cols + 2 * STEPS
    )
    kappa = stacked[kinds * level_rows :]
    for repeat in range(STEPS):
        trim = repeat
        coefficients = kappa[:, trim : kappa.shape[1] - trim, trim : kappa.shape[2] - trim]
        values = substep(values, coefficients)
        rim = STEPS - repeat - 1
        if rim:
            values = clear_outside(values, rim, lat_rows)
    return values


def network(features, w_first, w_middle, w_last):
    contract = (((0,), (0,)), ((), ()))
    hidden = jax.nn.gelu(
        lax.dot_general(w_first, features, contract, preferred_element_type=jnp.float32)
    ).astype(jnp.bfloat16)
    for layer_no in range(w_middle.shape[0]):
        hidden = jax.nn.gelu(
            lax.dot_general(
                w_middle[layer_no], hidden, contract, preferred_element_type=jnp.float32
            )
        ).astype(jnp.bfloat16)
    return lax.dot_general(w_last, hidden, contract, preferred_element_type=jnp.float32).astype(
        jnp.bfloat16
    )


def on_device(fields, diffusivity, cloudy_index, owners, w_in, w_mid, w_out):
    values = dynamics(fields, diffusivity)
    lev_count = lax.axis_size("lev")
    lon_count = lax.axis_size("lon")
    level_rows = values.shape[1]
    cells = values.shape[2] * values.shape[3]
    column_ids = cloudy_index[0]
    cloudy = column_ids.shape[0]
    per_device = cloudy // lev_count
    capacity = min(per_device, 4 * per_device // lon_count)
    feature_count = 2 * LEVELS
    flat_values = values.reshape(2 * level_rows, cells)
    picker = (column_ids[:, None] == jnp.arange(cells, dtype=jnp.int32)[None, :]).astype(
        jnp.bfloat16
    )
    picked = lax.dot_general(
        flat_values.astype(jnp.bfloat16),
        picker,
        (((1,), (1,)), ((), ())),
        preferred_element_type=jnp.float32,
    )
    picked = picked.astype(jnp.bfloat16).reshape(2, level_rows, cloudy)
    routes = owners[0, :, 0]
    pieces = routes.reshape(lev_count, per_device)
    onehot = (pieces[:, :, None] == jnp.arange(lon_count, dtype=jnp.int32)).astype(jnp.int32)
    slot_rank = jnp.sum(jnp.cumsum(onehot, 1) * onehot, 2) - 1
    columns = lax.all_to_all(picked, "lev", split_axis=2, concat_axis=1, tiled=True).reshape(
        feature_count, per_device
    )
    lev_pos = lax.axis_index("lev")
    my_route = lax.dynamic_index_in_dim(pieces, lev_pos, 0, keepdims=False)
    my_rank = lax.dynamic_index_in_dim(slot_rank, lev_pos, 0, keepdims=False)
    slot_index = my_route * capacity + my_rank
    send_buffer = (
        jnp.zeros((feature_count, lon_count * capacity), jnp.bfloat16)
        .at[:, slot_index]
        .set(columns)
    )
    send_buffer = send_buffer.reshape(feature_count, lon_count, capacity)
    received = lax.all_to_all(send_buffer, "lon", split_axis=1, concat_axis=1, tiled=True)
    outcome = network(received.reshape(feature_count, -1), w_in[0], w_mid[0], w_out[0]).reshape(
        received.shape
    )
    returned = lax.all_to_all(outcome, "lon", split_axis=1, concat_axis=1, tiled=True).reshape(
        feature_count, lon_count * capacity
    )
    returned = returned[:, slot_index].reshape(2, LEVELS, per_device)
    tendency = lax.all_to_all(returned, "lev", split_axis=1, concat_axis=2, tiled=True)
    spread = jnp.dot(
        tendency.reshape(2 * level_rows, cloudy), picker, preferred_element_type=jnp.float32
    )
    updated = flat_values + spread
    return updated.reshape(values.shape)


def solution(mesh):
    in_specs = (
        P(None, "lev", "lat", "lon"),
        P("lev", "lat", "lon"),
        P("lat", "lon"),
        P("lat", "lon", None),
        P("lon", None, None),
        P("lon", None, None, None),
        P("lon", None, None),
    )
    out_specs = P(None, "lev", "lat", "lon")
    return jax.shard_map(
        on_device, mesh=mesh, in_specs=in_specs, out_specs=out_specs, check_vma=False
    )
```

```python
import jax
import jax.numpy as jnp
from jax import lax
from jax.sharding import PartitionSpec as P

LEVELS = 60
STEPS = 3


def halo_exchange(cells, width):
    lat_count = lax.axis_size("lat")
    from_above = lax.ppermute(
        cells[..., cells.shape[-2] - width :, :], "lat", [(i, i + 1) for i in range(lat_count - 1)]
    )
    from_below = lax.ppermute(
        cells[..., :width, :], "lat", [(i + 1, i) for i in range(lat_count - 1)]
    )
    cells = jnp.concatenate([from_above, cells, from_below], axis=-2)
    lon_count = lax.axis_size("lon")
    left = cells[..., :width]
    right = cells[..., cells.shape[-1] - width :]
    if lon_count == 2:
        both = lax.ppermute(jnp.concatenate([right, left], axis=-1), "lon", [(0, 1), (1, 0)])
        from_left, from_right = both[..., :width], both[..., width:]
    else:
        from_left = lax.ppermute(right, "lon", [(i, (i + 1) % lon_count) for i in range(lon_count)])
        from_right = lax.ppermute(left, "lon", [((i + 1) % lon_count, i) for i in range(lon_count)])
    return jnp.concatenate([from_left, cells, from_right], axis=-1)


def substep(values, coefficients):
    centre = values[..., 1:-1, 1:-1]
    middle = coefficients[:, 1:-1, 1:-1]
    updated = centre
    for lat_cut, lon_cut in (
        (slice(0, -2), slice(1, -1)),
        (slice(2, None), slice(1, -1)),
        (slice(1, -1), slice(0, -2)),
        (slice(1, -1), slice(2, None)),
    ):
        neighbour = values[..., lat_cut, lon_cut]
        face_coef = 0.5 * (middle + coefficients[:, lat_cut, lon_cut])
        updated = updated + face_coef * (neighbour - centre)
    return updated


def clear_outside(values, rim_width, lat_rows):
    lat_pos = (
        lax.axis_index("lat") * lat_rows - rim_width + jnp.arange(values.shape[-2], dtype=jnp.int32)
    )
    inside = (lat_pos >= 0) & (lat_pos < lat_rows * lax.axis_size("lat"))
    return jnp.where(inside[:, None], values, 0.0)


def dynamics(fields, diffusivity):
    kinds, level_rows, lat_rows, lon_cols = fields.shape
    stacked = jnp.concatenate(
        [fields.reshape(kinds * level_rows, lat_rows, lon_cols), diffusivity], axis=0
    )
    stacked = halo_exchange(stacked, STEPS)
    values = stacked[: kinds * level_rows].reshape(
        kinds, level_rows, lat_rows + 2 * STEPS, lon_cols + 2 * STEPS
    )
    kappa = stacked[kinds * level_rows :]
    for repeat in range(STEPS):
        trim = repeat
        coefficients = kappa[:, trim : kappa.shape[1] - trim, trim : kappa.shape[2] - trim]
        values = substep(values, coefficients)
        rim = STEPS - repeat - 1
        if rim:
            values = clear_outside(values, rim, lat_rows)
    return values


def network(features, w_first, w_middle, w_last):
    contract = (((0,), (0,)), ((), ()))
    hidden = jax.nn.gelu(
        lax.dot_general(w_first, features, contract, preferred_element_type=jnp.float32)
    ).astype(jnp.bfloat16)
    for layer_no in range(w_middle.shape[0]):
        hidden = jax.nn.gelu(
            lax.dot_general(
                w_middle[layer_no], hidden, contract, preferred_element_type=jnp.float32
            )
        ).astype(jnp.bfloat16)
    return lax.dot_general(w_last, hidden, contract, preferred_element_type=jnp.float32).astype(
        jnp.bfloat16
    )


def on_device(fields, diffusivity, cloudy_index, owners, w_in, w_mid, w_out):
    values = dynamics(fields, diffusivity)
    lev_count = lax.axis_size("lev")
    lon_count = lax.axis_size("lon")
    level_rows = values.shape[1]
    cells = values.shape[2] * values.shape[3]
    column_ids = cloudy_index[0]
    cloudy = column_ids.shape[0]
    per_device = cloudy // lev_count
    capacity = min(per_device, 4 * per_device // lon_count)
    feature_count = 2 * LEVELS
    flat_values = values.reshape(2 * level_rows, cells)
    picker = (column_ids[:, None] == jnp.arange(cells, dtype=jnp.int32)[None, :]).astype(
        jnp.bfloat16
    )
    picked = lax.dot_general(
        flat_values.astype(jnp.bfloat16),
        picker,
        (((1,), (1,)), ((), ())),
        preferred_element_type=jnp.float32,
    )
    picked = picked.astype(jnp.bfloat16)
    routes = owners[0, :, 0]
    pieces = routes.reshape(lev_count, per_device)
    onehot = (pieces[:, :, None] == jnp.arange(lon_count, dtype=jnp.int32)).astype(jnp.int32)
    slot_rank = jnp.sum(jnp.cumsum(onehot, 1) * onehot, 2) - 1
    piece_of = jnp.arange(lev_count, dtype=jnp.int32)[:, None]
    slot_index = ((pieces * lev_count + piece_of) * capacity + slot_rank).reshape(cloudy)
    group = lon_count * lev_count
    local_features = 2 * level_rows
    send_buffer = (
        jnp.zeros((local_features, group * capacity), jnp.bfloat16)
        .at[:, slot_index]
        .set(picked)
    ).reshape(local_features, group, capacity)
    received = lax.all_to_all(
        send_buffer, ("lon", "lev"), split_axis=1, concat_axis=1, tiled=True
    )
    inputs = (
        received.reshape(2, level_rows, lon_count, lev_count, capacity)
        .transpose(0, 3, 1, 2, 4)
        .reshape(feature_count, lon_count * capacity)
    )
    outcome = network(inputs, w_in[0], w_mid[0], w_out[0])
    outgoing = (
        outcome.reshape(2, lev_count, level_rows, lon_count, capacity)
        .transpose(0, 2, 3, 1, 4)
        .reshape(local_features, group, capacity)
    )
    returned = lax.all_to_all(
        outgoing, ("lon", "lev"), split_axis=1, concat_axis=1, tiled=True
    ).reshape(local_features, group * capacity)
    tendency = returned[:, slot_index]
    spread = jnp.dot(
        tendency, picker, preferred_element_type=jnp.float32
    )
    updated = flat_values + spread
    return updated.reshape(values.shape)


def solution(mesh):
    in_specs = (
        P(None, "lev", "lat", "lon"),
        P("lev", "lat", "lon"),
        P("lat", "lon"),
        P("lat", "lon", None),
        P("lon", None, None),
        P("lon", None, None, None),
        P("lon", None, None),
    )
    out_specs = P(None, "lev", "lat", "lon")
    return jax.shard_map(
        on_device, mesh=mesh, in_specs=in_specs, out_specs=out_specs, check_vma=False
    )
```

```python
import jax
import jax.numpy as jnp
from jax import lax
from jax.sharding import PartitionSpec as P

LEVELS = 60
STEPS = 3


def halo_exchange(cells, width):
    lat_count = lax.axis_size("lat")
    from_above = lax.ppermute(
        cells[..., cells.shape[-2] - width :, :], "lat", [(i, i + 1) for i in range(lat_count - 1)]
    )
    from_below = lax.ppermute(
        cells[..., :width, :], "lat", [(i + 1, i) for i in range(lat_count - 1)]
    )
    cells = jnp.concatenate([from_above, cells, from_below], axis=-2)
    lon_count = lax.axis_size("lon")
    left = cells[..., :width]
    right = cells[..., cells.shape[-1] - width :]
    if lon_count == 2:
        both = lax.ppermute(jnp.concatenate([right, left], axis=-1), "lon", [(0, 1), (1, 0)])
        from_left, from_right = both[..., :width], both[..., width:]
    else:
        from_left = lax.ppermute(right, "lon", [(i, (i + 1) % lon_count) for i in range(lon_count)])
        from_right = lax.ppermute(left, "lon", [((i + 1) % lon_count, i) for i in range(lon_count)])
    return jnp.concatenate([from_left, cells, from_right], axis=-1)


def substep(values, coefficients):
    centre = values[..., 1:-1, 1:-1]
    middle = coefficients[:, 1:-1, 1:-1]
    updated = centre
    for lat_cut, lon_cut in (
        (slice(0, -2), slice(1, -1)),
        (slice(2, None), slice(1, -1)),
        (slice(1, -1), slice(0, -2)),
        (slice(1, -1), slice(2, None)),
    ):
        neighbour = values[..., lat_cut, lon_cut]
        face_coef = 0.5 * (middle + coefficients[:, lat_cut, lon_cut])
        updated = updated + face_coef * (neighbour - centre)
    return updated


def clear_outside(values, rim_width, lat_rows):
    lat_pos = (
        lax.axis_index("lat") * lat_rows - rim_width + jnp.arange(values.shape[-2], dtype=jnp.int32)
    )
    inside = (lat_pos >= 0) & (lat_pos < lat_rows * lax.axis_size("lat"))
    return jnp.where(inside[:, None], values, 0.0)


def dynamics(fields, diffusivity):
    kinds, level_rows, lat_rows, lon_cols = fields.shape
    stacked = jnp.concatenate(
        [fields.reshape(kinds * level_rows, lat_rows, lon_cols), diffusivity], axis=0
    )
    stacked = halo_exchange(stacked, STEPS)
    values = stacked[: kinds * level_rows].reshape(
        kinds, level_rows, lat_rows + 2 * STEPS, lon_cols + 2 * STEPS
    )
    kappa = stacked[kinds * level_rows :]
    for repeat in range(STEPS):
        trim = repeat
        coefficients = kappa[:, trim : kappa.shape[1] - trim, trim : kappa.shape[2] - trim]
        values = substep(values, coefficients)
        rim = STEPS - repeat - 1
        if rim:
            values = clear_outside(values, rim, lat_rows)
    return values


def network(features, w_first, w_middle, w_last):
    contract = (((0,), (0,)), ((), ()))
    hidden = jax.nn.gelu(
        lax.dot_general(w_first, features, contract, preferred_element_type=jnp.float32)
    ).astype(jnp.bfloat16)
    for layer_no in range(w_middle.shape[0]):
        hidden = jax.nn.gelu(
            lax.dot_general(
                w_middle[layer_no], hidden, contract, preferred_element_type=jnp.float32
            )
        ).astype(jnp.bfloat16)
    return lax.dot_general(w_last, hidden, contract, preferred_element_type=jnp.float32).astype(
        jnp.bfloat16
    )


def on_device(fields, diffusivity, cloudy_index, owners, w_in, w_mid, w_out):
    values = dynamics(fields, diffusivity)
    lev_count = lax.axis_size("lev")
    lon_count = lax.axis_size("lon")
    level_rows = values.shape[1]
    cells = values.shape[2] * values.shape[3]
    column_ids = cloudy_index[0]
    cloudy = column_ids.shape[0]
    per_device = cloudy // lev_count
    capacity = min(per_device, 4 * per_device // lon_count)
    feature_count = 2 * LEVELS
    flat_values = values.reshape(2 * level_rows, cells)
    picker = (column_ids[:, None] == jnp.arange(cells, dtype=jnp.int32)[None, :]).astype(
        jnp.bfloat16
    )
    picked = lax.dot_general(
        flat_values.astype(jnp.bfloat16),
        picker,
        (((1,), (1,)), ((), ())),
        preferred_element_type=jnp.float32,
    )
    picked = picked.astype(jnp.bfloat16)
    routes = owners[0, :, 0]
    group = lon_count * lev_count
    local_features = 2 * level_rows
    whole_slices = capacity == per_device
    if whole_slices:
        send_buffer = jnp.broadcast_to(
            picked.reshape(local_features, 1, lev_count, per_device),
            (local_features, lon_count, lev_count, per_device),
        ).reshape(local_features, group, capacity)
    else:
        pieces = routes.reshape(lev_count, per_device)
        onehot = (pieces[:, :, None] == jnp.arange(lon_count, dtype=jnp.int32)).astype(jnp.int32)
        slot_rank = jnp.sum(jnp.cumsum(onehot, 1) * onehot, 2) - 1
        piece_of = jnp.arange(lev_count, dtype=jnp.int32)[:, None]
        slot_index = ((pieces * lev_count + piece_of) * capacity + slot_rank).reshape(cloudy)
        send_buffer = (
            jnp.zeros((local_features, group * capacity), jnp.bfloat16)
            .at[:, slot_index]
            .set(picked)
        ).reshape(local_features, group, capacity)
    received = lax.all_to_all(
        send_buffer, ("lon", "lev"), split_axis=1, concat_axis=1, tiled=True
    )
    inputs = (
        received.reshape(2, level_rows, lon_count, lev_count, capacity)
        .transpose(0, 3, 1, 2, 4)
        .reshape(feature_count, lon_count * capacity)
    )
    outcome = network(inputs, w_in[0], w_mid[0], w_out[0])
    outgoing = (
        outcome.reshape(2, lev_count, level_rows, lon_count, capacity)
        .transpose(0, 2, 3, 1, 4)
        .reshape(local_features, group, capacity)
    )
    returned = lax.all_to_all(
        outgoing, ("lon", "lev"), split_axis=1, concat_axis=1, tiled=True
    )
    if whole_slices:
        returned = returned.reshape(local_features, lon_count, cloudy)
        tendency = returned[:, 0]
        for regime in range(1, lon_count):
            tendency = jnp.where(routes[None, :] == regime, returned[:, regime], tendency)
    else:
        tendency = returned.reshape(local_features, group * capacity)[:, slot_index]
    spread = jnp.dot(
        tendency, picker, preferred_element_type=jnp.float32
    )
    updated = flat_values + spread
    return updated.reshape(values.shape)


def solution(mesh):
    in_specs = (
        P(None, "lev", "lat", "lon"),
        P("lev", "lat", "lon"),
        P("lat", "lon"),
        P("lat", "lon", None),
        P("lon", None, None),
        P("lon", None, None, None),
        P("lon", None, None),
    )
    out_specs = P(None, "lev", "lat", "lon")
    return jax.shard_map(
        on_device, mesh=mesh, in_specs=in_specs, out_specs=out_specs, check_vma=False
    )
```

```python
import jax
import jax.numpy as jnp
from jax import lax
from jax.sharding import PartitionSpec as P

LEVELS = 60
STEPS = 3


def halo_exchange(cells, width):
    lat_count, lon_count = lax.axis_size("lat"), lax.axis_size("lon")
    rows, cols = cells.shape[-2], cells.shape[-1]
    top, bottom = cells[..., :width, :], cells[..., rows - width :, :]

    def lat_shift(piece, step):
        pairs = [(i, i + step) for i in range(lat_count) if 0 <= i + step < lat_count]
        return lax.ppermute(piece, "lat", pairs)

    def lon_shift(piece, step):
        pairs = [(j, (j + step) % lon_count) for j in range(lon_count)]
        return lax.ppermute(piece, "lon", pairs)

    def diagonal_shift(piece, lat_step, lon_step):
        pairs = [
            (i * lon_count + j, (i + lat_step) * lon_count + (j + lon_step) % lon_count)
            for i in range(lat_count)
            for j in range(lon_count)
            if 0 <= i + lat_step < lat_count
        ]
        return lax.ppermute(piece, ("lat", "lon"), pairs)

    def left_right(piece):
        return piece[..., :width], piece[..., cols - width :]

    north, south = lat_shift(bottom, 1), lat_shift(top, -1)
    left, right = left_right(cells)
    bottom_left, bottom_right = left_right(bottom)
    top_left, top_right = left_right(top)
    if lon_count == 2:
        west_east = lon_shift(jnp.concatenate([right, left], axis=-1), 1)
        west, east = west_east[..., :width], west_east[..., width:]
        upper = diagonal_shift(jnp.concatenate([bottom_right, bottom_left], axis=-1), 1, 1)
        north_west, north_east = upper[..., :width], upper[..., width:]
        lower = diagonal_shift(jnp.concatenate([top_right, top_left], axis=-1), -1, 1)
        south_west, south_east = lower[..., :width], lower[..., width:]
    else:
        west, east = lon_shift(right, 1), lon_shift(left, -1)
        north_west = diagonal_shift(bottom_right, 1, 1)
        north_east = diagonal_shift(bottom_left, 1, -1)
        south_west = diagonal_shift(top_right, -1, 1)
        south_east = diagonal_shift(top_left, -1, -1)
    return jnp.concatenate(
        [
            jnp.concatenate([north_west, north, north_east], axis=-1),
            jnp.concatenate([west, cells, east], axis=-1),
            jnp.concatenate([south_west, south, south_east], axis=-1),
        ],
        axis=-2,
    )


def substep(values, coefficients):
    centre = values[..., 1:-1, 1:-1]
    middle = coefficients[:, 1:-1, 1:-1]
    updated = centre
    for lat_cut, lon_cut in (
        (slice(0, -2), slice(1, -1)),
        (slice(2, None), slice(1, -1)),
        (slice(1, -1), slice(0, -2)),
        (slice(1, -1), slice(2, None)),
    ):
        neighbour = values[..., lat_cut, lon_cut]
        face_coef = 0.5 * (middle + coefficients[:, lat_cut, lon_cut])
        updated = updated + face_coef * (neighbour - centre)
    return updated


def clear_outside(values, rim_width, lat_rows):
    lat_pos = (
        lax.axis_index("lat") * lat_rows - rim_width + jnp.arange(values.shape[-2], dtype=jnp.int32)
    )
    inside = (lat_pos >= 0) & (lat_pos < lat_rows * lax.axis_size("lat"))
    return jnp.where(inside[:, None], values, 0.0)


def dynamics(fields, diffusivity):
    kinds, level_rows, lat_rows, lon_cols = fields.shape
    stacked = jnp.concatenate(
        [fields.reshape(kinds * level_rows, lat_rows, lon_cols), diffusivity], axis=0
    )
    stacked = halo_exchange(stacked, STEPS)
    values = stacked[: kinds * level_rows].reshape(
        kinds, level_rows, lat_rows + 2 * STEPS, lon_cols + 2 * STEPS
    )
    kappa = stacked[kinds * level_rows :]
    for repeat in range(STEPS):
        trim = repeat
        coefficients = kappa[:, trim : kappa.shape[1] - trim, trim : kappa.shape[2] - trim]
        values = substep(values, coefficients)
        rim = STEPS - repeat - 1
        if rim:
            values = clear_outside(values, rim, lat_rows)
    return values


def network(features, w_first, w_middle, w_last):
    contract = (((0,), (0,)), ((), ()))
    hidden = jax.nn.gelu(
        lax.dot_general(w_first, features, contract, preferred_element_type=jnp.float32)
    ).astype(jnp.bfloat16)
    for layer_no in range(w_middle.shape[0]):
        hidden = jax.nn.gelu(
            lax.dot_general(
                w_middle[layer_no], hidden, contract, preferred_element_type=jnp.float32
            )
        ).astype(jnp.bfloat16)
    return lax.dot_general(w_last, hidden, contract, preferred_element_type=jnp.float32).astype(
        jnp.bfloat16
    )


def on_device(fields, diffusivity, cloudy_index, owners, w_in, w_mid, w_out):
    values = dynamics(fields, diffusivity)
    lev_count = lax.axis_size("lev")
    lon_count = lax.axis_size("lon")
    level_rows = values.shape[1]
    cells = values.shape[2] * values.shape[3]
    column_ids = cloudy_index[0]
    cloudy = column_ids.shape[0]
    per_device = cloudy // lev_count
    capacity = min(per_device, 4 * per_device // lon_count)
    feature_count = 2 * LEVELS
    flat_values = values.reshape(2 * level_rows, cells)
    picker = (column_ids[:, None] == jnp.arange(cells, dtype=jnp.int32)[None, :]).astype(
        jnp.bfloat16
    )
    picked = lax.dot_general(
        flat_values.astype(jnp.bfloat16),
        picker,
        (((1,), (1,)), ((), ())),
        preferred_element_type=jnp.float32,
    )
    picked = picked.astype(jnp.bfloat16)
    routes = owners[0, :, 0]
    group = lon_count * lev_count
    local_features = 2 * level_rows
    whole_slices = capacity == per_device
    if whole_slices:
        send_buffer = jnp.broadcast_to(
            picked.reshape(local_features, 1, lev_count, per_device),
            (local_features, lon_count, lev_count, per_device),
        ).reshape(local_features, group, capacity)
    else:
        pieces = routes.reshape(lev_count, per_device)
        onehot = (pieces[:, :, None] == jnp.arange(lon_count, dtype=jnp.int32)).astype(jnp.int32)
        slot_rank = jnp.sum(jnp.cumsum(onehot, 1) * onehot, 2) - 1
        piece_of = jnp.arange(lev_count, dtype=jnp.int32)[:, None]
        slot_index = ((pieces * lev_count + piece_of) * capacity + slot_rank).reshape(cloudy)
        send_buffer = (
            jnp.zeros((local_features, group * capacity), jnp.bfloat16)
            .at[:, slot_index]
            .set(picked)
        ).reshape(local_features, group, capacity)
    received = lax.all_to_all(
        send_buffer, ("lon", "lev"), split_axis=1, concat_axis=1, tiled=True
    )
    inputs = (
        received.reshape(2, level_rows, lon_count, lev_count, capacity)
        .transpose(0, 3, 1, 2, 4)
        .reshape(feature_count, lon_count * capacity)
    )
    outcome = network(inputs, w_in[0], w_mid[0], w_out[0])
    outgoing = (
        outcome.reshape(2, lev_count, level_rows, lon_count, capacity)
        .transpose(0, 2, 3, 1, 4)
        .reshape(local_features, group, capacity)
    )
    returned = lax.all_to_all(
        outgoing, ("lon", "lev"), split_axis=1, concat_axis=1, tiled=True
    )
    if whole_slices:
        returned = returned.reshape(local_features, lon_count, cloudy)
        tendency = returned[:, 0]
        for regime in range(1, lon_count):
            tendency = jnp.where(routes[None, :] == regime, returned[:, regime], tendency)
    else:
        tendency = returned.reshape(local_features, group * capacity)[:, slot_index]
    spread = jnp.dot(
        tendency, picker, preferred_element_type=jnp.float32
    )
    updated = flat_values + spread
    return updated.reshape(values.shape)


def solution(mesh):
    in_specs = (
        P(None, "lev", "lat", "lon"),
        P("lev", "lat", "lon"),
        P("lat", "lon"),
        P("lat", "lon", None),
        P("lon", None, None),
        P("lon", None, None, None),
        P("lon", None, None),
    )
    out_specs = P(None, "lev", "lat", "lon")
    return jax.shard_map(
        on_device, mesh=mesh, in_specs=in_specs, out_specs=out_specs, check_vma=False
    )
```

```python
import jax
import jax.numpy as jnp
from jax import lax
from jax.sharding import PartitionSpec as P

LEVELS = 60
STEPS = 3


def halo_exchange(cells, width):
    lat_count = lax.axis_size("lat")
    from_above = lax.ppermute(
        cells[..., cells.shape[-2] - width :, :], "lat", [(i, i + 1) for i in range(lat_count - 1)]
    )
    from_below = lax.ppermute(
        cells[..., :width, :], "lat", [(i + 1, i) for i in range(lat_count - 1)]
    )
    cells = jnp.concatenate([from_above, cells, from_below], axis=-2)
    lon_count = lax.axis_size("lon")
    left = cells[..., :width]
    right = cells[..., cells.shape[-1] - width :]
    if lon_count == 2:
        both = lax.ppermute(jnp.concatenate([right, left], axis=-1), "lon", [(0, 1), (1, 0)])
        from_left, from_right = both[..., :width], both[..., width:]
    else:
        from_left = lax.ppermute(right, "lon", [(i, (i + 1) % lon_count) for i in range(lon_count)])
        from_right = lax.ppermute(left, "lon", [((i + 1) % lon_count, i) for i in range(lon_count)])
    return jnp.concatenate([from_left, cells, from_right], axis=-1)


def substep(values, coefficients):
    centre = values[..., 1:-1, 1:-1]
    middle = coefficients[:, 1:-1, 1:-1]
    updated = centre
    for lat_cut, lon_cut in (
        (slice(0, -2), slice(1, -1)),
        (slice(2, None), slice(1, -1)),
        (slice(1, -1), slice(0, -2)),
        (slice(1, -1), slice(2, None)),
    ):
        neighbour = values[..., lat_cut, lon_cut]
        face_coef = 0.5 * (middle + coefficients[:, lat_cut, lon_cut])
        updated = updated + face_coef * (neighbour - centre)
    return updated


def clear_outside(values, rim_width, lat_rows):
    lat_pos = (
        lax.axis_index("lat") * lat_rows - rim_width + jnp.arange(values.shape[-2], dtype=jnp.int32)
    )
    inside = (lat_pos >= 0) & (lat_pos < lat_rows * lax.axis_size("lat"))
    return jnp.where(inside[:, None], values, 0.0)


def dynamics(fields, diffusivity):
    kinds, level_rows, lat_rows, lon_cols = fields.shape
    stacked = jnp.concatenate(
        [fields.reshape(kinds * level_rows, lat_rows, lon_cols), diffusivity], axis=0
    )
    stacked = halo_exchange(stacked, STEPS)
    values = stacked[: kinds * level_rows].reshape(
        kinds, level_rows, lat_rows + 2 * STEPS, lon_cols + 2 * STEPS
    )
    kappa = stacked[kinds * level_rows :]
    for repeat in range(STEPS):
        trim = repeat
        coefficients = kappa[:, trim : kappa.shape[1] - trim, trim : kappa.shape[2] - trim]
        values = substep(values, coefficients)
        rim = STEPS - repeat - 1
        if rim:
            values = clear_outside(values, rim, lat_rows)
    return values


def network(features, w_first, w_middle, w_last):
    contract = (((0,), (0,)), ((), ()))
    hidden = jax.nn.gelu(
        lax.dot_general(w_first, features, contract, preferred_element_type=jnp.float32)
    ).astype(jnp.bfloat16)
    for layer_no in range(w_middle.shape[0]):
        hidden = jax.nn.gelu(
            lax.dot_general(
                w_middle[layer_no], hidden, contract, preferred_element_type=jnp.float32
            )
        ).astype(jnp.bfloat16)
    return lax.dot_general(w_last, hidden, contract, preferred_element_type=jnp.float32).astype(
        jnp.bfloat16
    )


def on_device(fields, diffusivity, cloudy_index, owners, w_in, w_mid, w_out):
    values = dynamics(fields, diffusivity)
    lev_count = lax.axis_size("lev")
    lon_count = lax.axis_size("lon")
    level_rows = values.shape[1]
    cells = values.shape[2] * values.shape[3]
    column_ids = cloudy_index[0]
    cloudy = column_ids.shape[0]
    per_device = cloudy // lev_count
    capacity = min(per_device, 4 * per_device // lon_count)
    feature_count = 2 * LEVELS
    lat_rows, lon_cols = values.shape[2], values.shape[3]
    local_features = 2 * level_rows
    planes = values.reshape(local_features, lat_rows, lon_cols)
    row_of = column_ids // lon_cols
    col_of = column_ids % lon_cols
    col_picker = (jnp.arange(lon_cols, dtype=jnp.int32)[:, None] == col_of[None, :]).astype(
        jnp.bfloat16
    )
    row_match = jnp.arange(lat_rows, dtype=jnp.int32)[:, None] == row_of[None, :]
    by_row = jnp.dot(
        planes.astype(jnp.bfloat16).reshape(local_features * lat_rows, lon_cols),
        col_picker,
        preferred_element_type=jnp.bfloat16,
    ).reshape(local_features, lat_rows, cloudy)
    picked = jnp.sum(jnp.where(row_match[None], by_row, jnp.zeros_like(by_row)), axis=1)
    routes = owners[0, :, 0]
    group = lon_count * lev_count
    whole_slices = capacity == per_device
    if whole_slices:
        send_buffer = jnp.broadcast_to(
            picked.reshape(local_features, 1, lev_count, per_device),
            (local_features, lon_count, lev_count, per_device),
        ).reshape(local_features, group, capacity)
    else:
        pieces = routes.reshape(lev_count, per_device)
        onehot = (pieces[:, :, None] == jnp.arange(lon_count, dtype=jnp.int32)).astype(jnp.int32)
        slot_rank = jnp.sum(jnp.cumsum(onehot, 1) * onehot, 2) - 1
        piece_of = jnp.arange(lev_count, dtype=jnp.int32)[:, None]
        slot_index = ((pieces * lev_count + piece_of) * capacity + slot_rank).reshape(cloudy)
        send_buffer = (
            jnp.zeros((local_features, group * capacity), jnp.bfloat16)
            .at[:, slot_index]
            .set(picked)
        ).reshape(local_features, group, capacity)
    received = lax.all_to_all(
        send_buffer, ("lon", "lev"), split_axis=1, concat_axis=1, tiled=True
    )
    inputs = (
        received.reshape(2, level_rows, lon_count, lev_count, capacity)
        .transpose(0, 3, 1, 2, 4)
        .reshape(feature_count, lon_count * capacity)
    )
    outcome = network(inputs, w_in[0], w_mid[0], w_out[0])
    outgoing = (
        outcome.reshape(2, lev_count, level_rows, lon_count, capacity)
        .transpose(0, 2, 3, 1, 4)
        .reshape(local_features, group, capacity)
    )
    returned = lax.all_to_all(
        outgoing, ("lon", "lev"), split_axis=1, concat_axis=1, tiled=True
    )
    if whole_slices:
        returned = returned.reshape(local_features, lon_count, cloudy)
        tendency = returned[:, 0]
        for regime in range(1, lon_count):
            tendency = jnp.where(routes[None, :] == regime, returned[:, regime], tendency)
    else:
        tendency = returned.reshape(local_features, group * capacity)[:, slot_index]
    spread_rows = jnp.where(row_match[None], tendency[:, None, :], jnp.zeros_like(tendency)[:, None, :])
    spread = lax.dot_general(
        spread_rows.reshape(local_features * lat_rows, cloudy),
        col_picker,
        (((1,), (1,)), ((), ())),
        preferred_element_type=jnp.float32,
    )
    updated = planes + spread.reshape(planes.shape)
    return updated.reshape(values.shape)


def solution(mesh):
    in_specs = (
        P(None, "lev", "lat", "lon"),
        P("lev", "lat", "lon"),
        P("lat", "lon"),
        P("lat", "lon", None),
        P("lon", None, None),
        P("lon", None, None, None),
        P("lon", None, None),
    )
    out_specs = P(None, "lev", "lat", "lon")
    return jax.shard_map(
        on_device, mesh=mesh, in_specs=in_specs, out_specs=out_specs, check_vma=False
    )
```

```python
import jax
import jax.numpy as jnp
from jax import lax
from jax.sharding import PartitionSpec as P

LEVELS = 60
STEPS = 3


def dense_ppermute(piece, axis, pairs):
    flat = piece.reshape(piece.shape[0], -1)
    return lax.ppermute(flat, axis, pairs).reshape(piece.shape)


def halo_exchange(cells, width):
    lat_count = lax.axis_size("lat")
    from_above = dense_ppermute(
        cells[..., cells.shape[-2] - width :, :], "lat", [(i, i + 1) for i in range(lat_count - 1)]
    )
    from_below = dense_ppermute(
        cells[..., :width, :], "lat", [(i + 1, i) for i in range(lat_count - 1)]
    )
    cells = jnp.concatenate([from_above, cells, from_below], axis=-2)
    lon_count = lax.axis_size("lon")
    left = cells[..., :width]
    right = cells[..., cells.shape[-1] - width :]
    if lon_count == 2:
        both = dense_ppermute(jnp.concatenate([right, left], axis=-1), "lon", [(0, 1), (1, 0)])
        from_left, from_right = both[..., :width], both[..., width:]
    else:
        from_left = dense_ppermute(
            right, "lon", [(i, (i + 1) % lon_count) for i in range(lon_count)]
        )
        from_right = dense_ppermute(
            left, "lon", [((i + 1) % lon_count, i) for i in range(lon_count)]
        )
    return jnp.concatenate([from_left, cells, from_right], axis=-1)


def substep(values, coefficients):
    centre = values[..., 1:-1, 1:-1]
    middle = coefficients[:, 1:-1, 1:-1]
    updated = centre
    for lat_cut, lon_cut in (
        (slice(0, -2), slice(1, -1)),
        (slice(2, None), slice(1, -1)),
        (slice(1, -1), slice(0, -2)),
        (slice(1, -1), slice(2, None)),
    ):
        neighbour = values[..., lat_cut, lon_cut]
        face_coef = 0.5 * (middle + coefficients[:, lat_cut, lon_cut])
        updated = updated + face_coef * (neighbour - centre)
    return updated


def clear_outside(values, rim_width, lat_rows):
    lat_pos = (
        lax.axis_index("lat") * lat_rows - rim_width + jnp.arange(values.shape[-2], dtype=jnp.int32)
    )
    inside = (lat_pos >= 0) & (lat_pos < lat_rows * lax.axis_size("lat"))
    return jnp.where(inside[:, None], values, 0.0)


def dynamics(fields, diffusivity):
    kinds, level_rows, lat_rows, lon_cols = fields.shape
    stacked = jnp.concatenate(
        [fields.reshape(kinds * level_rows, lat_rows, lon_cols), diffusivity], axis=0
    )
    stacked = halo_exchange(stacked, STEPS)
    values = stacked[: kinds * level_rows].reshape(
        kinds, level_rows, lat_rows + 2 * STEPS, lon_cols + 2 * STEPS
    )
    kappa = stacked[kinds * level_rows :]
    for repeat in range(STEPS):
        trim = repeat
        coefficients = kappa[:, trim : kappa.shape[1] - trim, trim : kappa.shape[2] - trim]
        values = substep(values, coefficients)
        rim = STEPS - repeat - 1
        if rim:
            values = clear_outside(values, rim, lat_rows)
    return values


def network(features, w_first, w_middle, w_last):
    contract = (((0,), (0,)), ((), ()))
    hidden = jax.nn.gelu(
        lax.dot_general(w_first, features, contract, preferred_element_type=jnp.float32)
    ).astype(jnp.bfloat16)
    for layer_no in range(w_middle.shape[0]):
        hidden = jax.nn.gelu(
            lax.dot_general(
                w_middle[layer_no], hidden, contract, preferred_element_type=jnp.float32
            )
        ).astype(jnp.bfloat16)
    return lax.dot_general(w_last, hidden, contract, preferred_element_type=jnp.float32).astype(
        jnp.bfloat16
    )


def on_device(fields, diffusivity, cloudy_index, owners, w_in, w_mid, w_out):
    values = dynamics(fields, diffusivity)
    lev_count = lax.axis_size("lev")
    lon_count = lax.axis_size("lon")
    level_rows = values.shape[1]
    cells = values.shape[2] * values.shape[3]
    column_ids = cloudy_index[0]
    cloudy = column_ids.shape[0]
    per_device = cloudy // lev_count
    capacity = min(per_device, 4 * per_device // lon_count)
    feature_count = 2 * LEVELS
    lat_rows, lon_cols = values.shape[2], values.shape[3]
    local_features = 2 * level_rows
    planes = values.reshape(local_features, lat_rows, lon_cols)
    row_of = column_ids // lon_cols
    col_of = column_ids % lon_cols
    col_picker = (jnp.arange(lon_cols, dtype=jnp.int32)[:, None] == col_of[None, :]).astype(
        jnp.bfloat16
    )
    row_match = jnp.arange(lat_rows, dtype=jnp.int32)[:, None] == row_of[None, :]
    by_row = jnp.dot(
        planes.astype(jnp.bfloat16).reshape(local_features * lat_rows, lon_cols),
        col_picker,
        preferred_element_type=jnp.bfloat16,
    ).reshape(local_features, lat_rows, cloudy)
    picked = jnp.sum(jnp.where(row_match[None], by_row, jnp.zeros_like(by_row)), axis=1)
    routes = owners[0, :, 0]
    group = lon_count * lev_count
    whole_slices = capacity == per_device
    if whole_slices:
        send_buffer = jnp.broadcast_to(
            picked.reshape(local_features, 1, lev_count, per_device),
            (local_features, lon_count, lev_count, per_device),
        ).reshape(local_features, group, capacity)
    else:
        pieces = routes.reshape(lev_count, per_device)
        onehot = (pieces[:, :, None] == jnp.arange(lon_count, dtype=jnp.int32)).astype(jnp.int32)
        slot_rank = jnp.sum(jnp.cumsum(onehot, 1) * onehot, 2) - 1
        piece_of = jnp.arange(lev_count, dtype=jnp.int32)[:, None]
        slot_index = ((pieces * lev_count + piece_of) * capacity + slot_rank).reshape(cloudy)
        send_buffer = (
            jnp.zeros((local_features, group * capacity), jnp.bfloat16)
            .at[:, slot_index]
            .set(picked)
        ).reshape(local_features, group, capacity)
    received = lax.all_to_all(
        send_buffer, ("lon", "lev"), split_axis=1, concat_axis=1, tiled=True
    )
    inputs = (
        received.reshape(2, level_rows, lon_count, lev_count, capacity)
        .transpose(0, 3, 1, 2, 4)
        .reshape(feature_count, lon_count * capacity)
    )
    outcome = network(inputs, w_in[0], w_mid[0], w_out[0])
    outgoing = (
        outcome.reshape(2, lev_count, level_rows, lon_count, capacity)
        .transpose(0, 2, 3, 1, 4)
        .reshape(local_features, group, capacity)
    )
    returned = lax.all_to_all(
        outgoing, ("lon", "lev"), split_axis=1, concat_axis=1, tiled=True
    )
    if whole_slices:
        returned = returned.reshape(local_features, lon_count, cloudy)
        tendency = returned[:, 0]
        for regime in range(1, lon_count):
            tendency = jnp.where(routes[None, :] == regime, returned[:, regime], tendency)
    else:
        tendency = returned.reshape(local_features, group * capacity)[:, slot_index]
    spread_rows = jnp.where(row_match[None], tendency[:, None, :], jnp.zeros_like(tendency)[:, None, :])
    spread = lax.dot_general(
        spread_rows.reshape(local_features * lat_rows, cloudy),
        col_picker,
        (((1,), (1,)), ((), ())),
        preferred_element_type=jnp.float32,
    )
    updated = planes + spread.reshape(planes.shape)
    return updated.reshape(values.shape)


def solution(mesh):
    in_specs = (
        P(None, "lev", "lat", "lon"),
        P("lev", "lat", "lon"),
        P("lat", "lon"),
        P("lat", "lon", None),
        P("lon", None, None),
        P("lon", None, None, None),
        P("lon", None, None),
    )
    out_specs = P(None, "lev", "lat", "lon")
    return jax.shard_map(
        on_device, mesh=mesh, in_specs=in_specs, out_specs=out_specs, check_vma=False
    )
```

```python
import jax
import jax.numpy as jnp
from jax import lax
from jax.sharding import PartitionSpec as P

LEVELS = 60
STEPS = 3


def dense_ppermute(piece, axis, pairs):
    flat = piece.reshape(piece.shape[0], -1)
    return lax.ppermute(flat, axis, pairs).reshape(piece.shape)


def lat_exchange(cells, width):
    lat_count = lax.axis_size("lat")
    from_above = dense_ppermute(
        cells[..., cells.shape[-2] - width :, :], "lat", [(i, i + 1) for i in range(lat_count - 1)]
    )
    from_below = dense_ppermute(
        cells[..., :width, :], "lat", [(i + 1, i) for i in range(lat_count - 1)]
    )
    return jnp.concatenate([from_above, cells, from_below], axis=-2)


def lon_exchange(cells, width):
    lon_count = lax.axis_size("lon")
    left = cells[..., :width]
    right = cells[..., cells.shape[-1] - width :]
    if lon_count == 2:
        both = dense_ppermute(jnp.concatenate([right, left], axis=-1), "lon", [(0, 1), (1, 0)])
        return both[..., :width], both[..., width:]
    from_left = dense_ppermute(right, "lon", [(i, (i + 1) % lon_count) for i in range(lon_count)])
    from_right = dense_ppermute(left, "lon", [((i + 1) % lon_count, i) for i in range(lon_count)])
    return from_left, from_right


def substep(values, coefficients):
    centre = values[..., 1:-1, 1:-1]
    middle = coefficients[:, 1:-1, 1:-1]
    updated = centre
    for lat_cut, lon_cut in (
        (slice(0, -2), slice(1, -1)),
        (slice(2, None), slice(1, -1)),
        (slice(1, -1), slice(0, -2)),
        (slice(1, -1), slice(2, None)),
    ):
        neighbour = values[..., lat_cut, lon_cut]
        face_coef = 0.5 * (middle + coefficients[:, lat_cut, lon_cut])
        updated = updated + face_coef * (neighbour - centre)
    return updated


def clear_outside(values, rim_width, lat_rows):
    lat_pos = (
        lax.axis_index("lat") * lat_rows - rim_width + jnp.arange(values.shape[-2], dtype=jnp.int32)
    )
    inside = (lat_pos >= 0) & (lat_pos < lat_rows * lax.axis_size("lat"))
    return jnp.where(inside[:, None], values, 0.0)


def run_steps(stacked, kinds, level_rows, lat_rows):
    values = stacked[: kinds * level_rows].reshape(
        (kinds, level_rows) + stacked.shape[1:]
    )
    kappa = stacked[kinds * level_rows :]
    for repeat in range(STEPS):
        trim = repeat
        coefficients = kappa[:, trim : kappa.shape[1] - trim, trim : kappa.shape[2] - trim]
        values = substep(values, coefficients)
        rim = STEPS - repeat - 1
        if rim:
            values = clear_outside(values, rim, lat_rows)
    return values


def dynamics(fields, diffusivity):
    kinds, level_rows, lat_rows, lon_cols = fields.shape
    stacked = jnp.concatenate(
        [fields.reshape(kinds * level_rows, lat_rows, lon_cols), diffusivity], axis=0
    )
    stacked = lat_exchange(stacked, STEPS)
    from_left, from_right = lon_exchange(stacked, STEPS)
    interior = run_steps(stacked, kinds, level_rows, lat_rows)
    left_strip = jnp.concatenate([from_left, stacked[..., : 2 * STEPS]], axis=-1)
    right_strip = jnp.concatenate([stacked[..., lon_cols - 2 * STEPS :], from_right], axis=-1)
    left_part = run_steps(left_strip, kinds, level_rows, lat_rows)
    right_part = run_steps(right_strip, kinds, level_rows, lat_rows)
    return jnp.concatenate([left_part, interior, right_part], axis=-1)


def network(features, w_first, w_middle, w_last):
    contract = (((0,), (0,)), ((), ()))
    hidden = jax.nn.gelu(
        lax.dot_general(w_first, features, contract, preferred_element_type=jnp.float32)
    ).astype(jnp.bfloat16)
    for layer_no in range(w_middle.shape[0]):
        hidden = jax.nn.gelu(
            lax.dot_general(
                w_middle[layer_no], hidden, contract, preferred_element_type=jnp.float32
            )
        ).astype(jnp.bfloat16)
    return lax.dot_general(w_last, hidden, contract, preferred_element_type=jnp.float32).astype(
        jnp.bfloat16
    )


def on_device(fields, diffusivity, cloudy_index, owners, w_in, w_mid, w_out):
    values = dynamics(fields, diffusivity)
    lev_count = lax.axis_size("lev")
    lon_count = lax.axis_size("lon")
    level_rows = values.shape[1]
    cells = values.shape[2] * values.shape[3]
    column_ids = cloudy_index[0]
    cloudy = column_ids.shape[0]
    per_device = cloudy // lev_count
    capacity = min(per_device, 4 * per_device // lon_count)
    feature_count = 2 * LEVELS
    lat_rows, lon_cols = values.shape[2], values.shape[3]
    local_features = 2 * level_rows
    planes = values.reshape(local_features, lat_rows, lon_cols)
    row_of = column_ids // lon_cols
    col_of = column_ids % lon_cols
    col_picker = (jnp.arange(lon_cols, dtype=jnp.int32)[:, None] == col_of[None, :]).astype(
        jnp.bfloat16
    )
    row_match = jnp.arange(lat_rows, dtype=jnp.int32)[:, None] == row_of[None, :]
    by_row = jnp.dot(
        planes.astype(jnp.bfloat16).reshape(local_features * lat_rows, lon_cols),
        col_picker,
        preferred_element_type=jnp.bfloat16,
    ).reshape(local_features, lat_rows, cloudy)
    picked = jnp.sum(jnp.where(row_match[None], by_row, jnp.zeros_like(by_row)), axis=1)
    routes = owners[0, :, 0]
    group = lon_count * lev_count
    whole_slices = capacity == per_device
    if whole_slices:
        send_buffer = jnp.broadcast_to(
            picked.reshape(local_features, 1, lev_count, per_device),
            (local_features, lon_count, lev_count, per_device),
        ).reshape(local_features, group, capacity)
    else:
        pieces = routes.reshape(lev_count, per_device)
        onehot = (pieces[:, :, None] == jnp.arange(lon_count, dtype=jnp.int32)).astype(jnp.int32)
        slot_rank = jnp.sum(jnp.cumsum(onehot, 1) * onehot, 2) - 1
        piece_of = jnp.arange(lev_count, dtype=jnp.int32)[:, None]
        slot_index = ((pieces * lev_count + piece_of) * capacity + slot_rank).reshape(cloudy)
        send_buffer = (
            jnp.zeros((local_features, group * capacity), jnp.bfloat16)
            .at[:, slot_index]
            .set(picked)
        ).reshape(local_features, group, capacity)
    received = lax.all_to_all(
        send_buffer, ("lon", "lev"), split_axis=1, concat_axis=1, tiled=True
    )
    inputs = (
        received.reshape(2, level_rows, lon_count, lev_count, capacity)
        .transpose(0, 3, 1, 2, 4)
        .reshape(feature_count, lon_count * capacity)
    )
    outcome = network(inputs, w_in[0], w_mid[0], w_out[0])
    outgoing = (
        outcome.reshape(2, lev_count, level_rows, lon_count, capacity)
        .transpose(0, 2, 3, 1, 4)
        .reshape(local_features, group, capacity)
    )
    returned = lax.all_to_all(
        outgoing, ("lon", "lev"), split_axis=1, concat_axis=1, tiled=True
    )
    if whole_slices:
        returned = returned.reshape(local_features, lon_count, cloudy)
        tendency = returned[:, 0]
        for regime in range(1, lon_count):
            tendency = jnp.where(routes[None, :] == regime, returned[:, regime], tendency)
    else:
        tendency = returned.reshape(local_features, group * capacity)[:, slot_index]
    spread_rows = jnp.where(row_match[None], tendency[:, None, :], jnp.zeros_like(tendency)[:, None, :])
    spread = lax.dot_general(
        spread_rows.reshape(local_features * lat_rows, cloudy),
        col_picker,
        (((1,), (1,)), ((), ())),
        preferred_element_type=jnp.float32,
    )
    updated = planes + spread.reshape(planes.shape)
    return updated.reshape(values.shape)


def solution(mesh):
    in_specs = (
        P(None, "lev", "lat", "lon"),
        P("lev", "lat", "lon"),
        P("lat", "lon"),
        P("lat", "lon", None),
        P("lon", None, None),
        P("lon", None, None, None),
        P("lon", None, None),
    )
    out_specs = P(None, "lev", "lat", "lon")
    return jax.shard_map(
        on_device, mesh=mesh, in_specs=in_specs, out_specs=out_specs, check_vma=False
    )
```

```python
import jax
import jax.numpy as jnp
from jax import lax
from jax.sharding import PartitionSpec as P

LEVELS = 60
STEPS = 3


def halo_exchange(cells, width):
    lat_count = lax.axis_size("lat")
    from_above = lax.ppermute(
        cells[..., cells.shape[-2] - width :, :], "lat", [(i, i + 1) for i in range(lat_count - 1)]
    )
    from_below = lax.ppermute(
        cells[..., :width, :], "lat", [(i + 1, i) for i in range(lat_count - 1)]
    )
    cells = jnp.concatenate([from_above, cells, from_below], axis=-2)
    lon_count = lax.axis_size("lon")
    left = cells[..., :width]
    right = cells[..., cells.shape[-1] - width :]
    if lon_count == 2:
        both = lax.ppermute(jnp.concatenate([right, left], axis=-1), "lon", [(0, 1), (1, 0)])
        from_left, from_right = both[..., :width], both[..., width:]
    else:
        from_left = lax.ppermute(right, "lon", [(i, (i + 1) % lon_count) for i in range(lon_count)])
        from_right = lax.ppermute(left, "lon", [((i + 1) % lon_count, i) for i in range(lon_count)])
    return jnp.concatenate([from_left, cells, from_right], axis=-1)


def substep(values, coefficients):
    centre = values[..., 1:-1, 1:-1]
    middle = coefficients[:, 1:-1, 1:-1]
    updated = centre
    for lat_cut, lon_cut in (
        (slice(0, -2), slice(1, -1)),
        (slice(2, None), slice(1, -1)),
        (slice(1, -1), slice(0, -2)),
        (slice(1, -1), slice(2, None)),
    ):
        neighbour = values[..., lat_cut, lon_cut]
        face_coef = 0.5 * (middle + coefficients[:, lat_cut, lon_cut])
        updated = updated + face_coef * (neighbour - centre)
    return updated


def clear_outside(values, rim_width, lat_rows):
    lat_pos = (
        lax.axis_index("lat") * lat_rows - rim_width + jnp.arange(values.shape[-2], dtype=jnp.int32)
    )
    inside = (lat_pos >= 0) & (lat_pos < lat_rows * lax.axis_size("lat"))
    return jnp.where(inside[:, None], values, 0.0)


def dynamics(fields, diffusivity):
    kinds, level_rows, lat_rows, lon_cols = fields.shape
    planes = fields.reshape(kinds * level_rows, lat_rows, lon_cols)
    lat_count, lon_count = lax.axis_size("lat"), lax.axis_size("lon")
    width = STEPS

    def both(cut):
        return jnp.concatenate([planes[cut], diffusivity[cut]], axis=0)

    bottom_rows = both((slice(None), slice(lat_rows - width, None)))
    top_rows = both((slice(None), slice(0, width)))
    north = lax.ppermute(bottom_rows, "lat", [(i, i + 1) for i in range(lat_count - 1)])
    south = lax.ppermute(top_rows, "lat", [(i + 1, i) for i in range(lat_count - 1)])

    def edge(cut):
        return jnp.concatenate([north[..., cut], both((slice(None), slice(None), cut)), south[..., cut]], axis=-2)

    left, right = edge(slice(0, width)), edge(slice(lon_cols - width, None))
    if lon_count == 2:
        swapped = lax.ppermute(jnp.concatenate([right, left], axis=-1), "lon", [(0, 1), (1, 0)])
        west, east = swapped[..., :width], swapped[..., width:]
    else:
        west = lax.ppermute(right, "lon", [(i, (i + 1) % lon_count) for i in range(lon_count)])
        east = lax.ppermute(left, "lon", [((i + 1) % lon_count, i) for i in range(lon_count)])
    count = kinds * level_rows

    def assemble(own, first, last):
        middle = jnp.concatenate([north[first:last], own, south[first:last]], axis=-2)
        return jnp.concatenate([west[first:last], middle, east[first:last]], axis=-1)

    values = assemble(planes, 0, count).reshape(
        kinds, level_rows, lat_rows + 2 * width, lon_cols + 2 * width
    )
    kappa = assemble(diffusivity, count, count + diffusivity.shape[0])
    for repeat in range(STEPS):
        trim = repeat
        coefficients = kappa[:, trim : kappa.shape[1] - trim, trim : kappa.shape[2] - trim]
        values = substep(values, coefficients)
        rim = STEPS - repeat - 1
        if rim:
            values = clear_outside(values, rim, lat_rows)
    return values


def network(features, w_first, w_middle, w_last):
    contract = (((0,), (0,)), ((), ()))
    hidden = jax.nn.gelu(
        lax.dot_general(w_first, features, contract, preferred_element_type=jnp.float32)
    ).astype(jnp.bfloat16)
    for layer_no in range(w_middle.shape[0]):
        hidden = jax.nn.gelu(
            lax.dot_general(
                w_middle[layer_no], hidden, contract, preferred_element_type=jnp.float32
            )
        ).astype(jnp.bfloat16)
    return lax.dot_general(w_last, hidden, contract, preferred_element_type=jnp.float32).astype(
        jnp.bfloat16
    )


def on_device(fields, diffusivity, cloudy_index, owners, w_in, w_mid, w_out):
    values = dynamics(fields, diffusivity)
    lev_count = lax.axis_size("lev")
    lon_count = lax.axis_size("lon")
    level_rows = values.shape[1]
    cells = values.shape[2] * values.shape[3]
    column_ids = cloudy_index[0]
    cloudy = column_ids.shape[0]
    per_device = cloudy // lev_count
    capacity = min(per_device, 4 * per_device // lon_count)
    feature_count = 2 * LEVELS
    lat_rows, lon_cols = values.shape[2], values.shape[3]
    local_features = 2 * level_rows
    planes = values.reshape(local_features, lat_rows, lon_cols)
    row_of = column_ids // lon_cols
    col_of = column_ids % lon_cols
    col_picker = (jnp.arange(lon_cols, dtype=jnp.int32)[:, None] == col_of[None, :]).astype(
        jnp.bfloat16
    )
    row_match = jnp.arange(lat_rows, dtype=jnp.int32)[:, None] == row_of[None, :]
    by_row = jnp.dot(
        planes.astype(jnp.bfloat16).reshape(local_features * lat_rows, lon_cols),
        col_picker,
        preferred_element_type=jnp.bfloat16,
    ).reshape(local_features, lat_rows, cloudy)
    picked = jnp.sum(jnp.where(row_match[None], by_row, jnp.zeros_like(by_row)), axis=1)
    routes = owners[0, :, 0]
    group = lon_count * lev_count
    whole_slices = capacity == per_device
    if whole_slices:
        send_buffer = jnp.broadcast_to(
            picked.reshape(local_features, 1, lev_count, per_device),
            (local_features, lon_count, lev_count, per_device),
        ).reshape(local_features, group, capacity)
    else:
        pieces = routes.reshape(lev_count, per_device)
        onehot = (pieces[:, :, None] == jnp.arange(lon_count, dtype=jnp.int32)).astype(jnp.int32)
        slot_rank = jnp.sum(jnp.cumsum(onehot, 1) * onehot, 2) - 1
        piece_of = jnp.arange(lev_count, dtype=jnp.int32)[:, None]
        slot_index = ((pieces * lev_count + piece_of) * capacity + slot_rank).reshape(cloudy)
        send_buffer = (
            jnp.zeros((local_features, group * capacity), jnp.bfloat16)
            .at[:, slot_index]
            .set(picked)
        ).reshape(local_features, group, capacity)
    received = lax.all_to_all(
        send_buffer, ("lon", "lev"), split_axis=1, concat_axis=1, tiled=True
    )
    inputs = (
        received.reshape(2, level_rows, lon_count, lev_count, capacity)
        .transpose(0, 3, 1, 2, 4)
        .reshape(feature_count, lon_count * capacity)
    )
    outcome = network(inputs, w_in[0], w_mid[0], w_out[0])
    outgoing = (
        outcome.reshape(2, lev_count, level_rows, lon_count, capacity)
        .transpose(0, 2, 3, 1, 4)
        .reshape(local_features, group, capacity)
    )
    returned = lax.all_to_all(
        outgoing, ("lon", "lev"), split_axis=1, concat_axis=1, tiled=True
    )
    if whole_slices:
        returned = returned.reshape(local_features, lon_count, cloudy)
        tendency = returned[:, 0]
        for regime in range(1, lon_count):
            tendency = jnp.where(routes[None, :] == regime, returned[:, regime], tendency)
    else:
        tendency = returned.reshape(local_features, group * capacity)[:, slot_index]
    spread_rows = jnp.where(row_match[None], tendency[:, None, :], jnp.zeros_like(tendency)[:, None, :])
    spread = lax.dot_general(
        spread_rows.reshape(local_features * lat_rows, cloudy),
        col_picker,
        (((1,), (1,)), ((), ())),
        preferred_element_type=jnp.float32,
    )
    updated = planes + spread.reshape(planes.shape)
    return updated.reshape(values.shape)


def solution(mesh):
    in_specs = (
        P(None, "lev", "lat", "lon"),
        P("lev", "lat", "lon"),
        P("lat", "lon"),
        P("lat", "lon", None),
        P("lon", None, None),
        P("lon", None, None, None),
        P("lon", None, None),
    )
    out_specs = P(None, "lev", "lat", "lon")
    return jax.shard_map(
        on_device, mesh=mesh, in_specs=in_specs, out_specs=out_specs, check_vma=False
    )
```

```python
import jax
import jax.numpy as jnp
from jax import lax
from jax.sharding import PartitionSpec as P

LEVELS = 60
STEPS = 3


def halo_exchange(cells, width):
    lat_count = lax.axis_size("lat")
    from_above = lax.ppermute(
        cells[..., cells.shape[-2] - width :, :], "lat", [(i, i + 1) for i in range(lat_count - 1)]
    )
    from_below = lax.ppermute(
        cells[..., :width, :], "lat", [(i + 1, i) for i in range(lat_count - 1)]
    )
    cells = jnp.concatenate([from_above, cells, from_below], axis=-2)
    lon_count = lax.axis_size("lon")
    left = cells[..., :width]
    right = cells[..., cells.shape[-1] - width :]
    if lon_count == 2:
        both = lax.ppermute(jnp.stack([right, left]), "lon", [(0, 1), (1, 0)])
        from_left, from_right = both[0], both[1]
    else:
        from_left = lax.ppermute(right, "lon", [(i, (i + 1) % lon_count) for i in range(lon_count)])
        from_right = lax.ppermute(left, "lon", [((i + 1) % lon_count, i) for i in range(lon_count)])
    return jnp.concatenate([from_left, cells, from_right], axis=-1)


NEIGHBOURS = (
    (slice(0, -2), slice(1, -1)),
    (slice(2, None), slice(1, -1)),
    (slice(1, -1), slice(0, -2)),
    (slice(1, -1), slice(2, None)),
)


def face_coefficients(coefficients):
    middle = coefficients[:, 1:-1, 1:-1]
    return [0.5 * (middle + coefficients[:, lat_cut, lon_cut]) for lat_cut, lon_cut in NEIGHBOURS]


def substep(values, faces):
    centre = values[..., 1:-1, 1:-1]
    updated = centre
    for (lat_cut, lon_cut), face_coef in zip(NEIGHBOURS, faces):
        neighbour = values[..., lat_cut, lon_cut]
        updated = updated + face_coef * (neighbour - centre)
    return updated


def clear_outside(values, rim_width, lat_rows):
    lat_pos = (
        lax.axis_index("lat") * lat_rows - rim_width + jnp.arange(values.shape[-2], dtype=jnp.int32)
    )
    inside = (lat_pos >= 0) & (lat_pos < lat_rows * lax.axis_size("lat"))
    return jnp.where(inside[:, None], values, 0.0)


def dynamics(fields, diffusivity):
    kinds, level_rows, lat_rows, lon_cols = fields.shape
    stacked = jnp.concatenate(
        [fields.reshape(kinds * level_rows, lat_rows, lon_cols), diffusivity], axis=0
    )
    stacked = halo_exchange(stacked, STEPS)
    values = stacked[: kinds * level_rows].reshape(
        kinds, level_rows, lat_rows + 2 * STEPS, lon_cols + 2 * STEPS
    )
    kappa = stacked[kinds * level_rows :]
    faces = face_coefficients(kappa)
    for repeat in range(STEPS):
        trim = repeat
        values = substep(
            values, [f[:, trim : f.shape[1] - trim, trim : f.shape[2] - trim] for f in faces]
        )
        rim = STEPS - repeat - 1
        if rim:
            values = clear_outside(values, rim, lat_rows)
    return values


def network(features, w_first, w_middle, w_last):
    contract = (((0,), (0,)), ((), ()))
    hidden = jax.nn.gelu(
        lax.dot_general(w_first, features, contract, preferred_element_type=jnp.float32)
    ).astype(jnp.bfloat16)
    for layer_no in range(w_middle.shape[0]):
        hidden = jax.nn.gelu(
            lax.dot_general(
                w_middle[layer_no], hidden, contract, preferred_element_type=jnp.float32
            )
        ).astype(jnp.bfloat16)
    return lax.dot_general(w_last, hidden, contract, preferred_element_type=jnp.float32).astype(
        jnp.bfloat16
    )


def on_device(fields, diffusivity, cloudy_index, owners, w_in, w_mid, w_out):
    values = dynamics(fields, diffusivity)
    lev_count = lax.axis_size("lev")
    lon_count = lax.axis_size("lon")
    level_rows = values.shape[1]
    cells = values.shape[2] * values.shape[3]
    column_ids = cloudy_index[0]
    cloudy = column_ids.shape[0]
    per_device = cloudy // lev_count
    capacity = min(per_device, 4 * per_device // lon_count)
    feature_count = 2 * LEVELS
    lat_rows, lon_cols = values.shape[2], values.shape[3]
    local_features = 2 * level_rows
    planes = values.reshape(local_features, lat_rows, lon_cols)
    row_of = column_ids // lon_cols
    col_of = column_ids % lon_cols
    col_picker = (jnp.arange(lon_cols, dtype=jnp.int32)[:, None] == col_of[None, :]).astype(
        jnp.bfloat16
    )
    row_match = jnp.arange(lat_rows, dtype=jnp.int32)[:, None] == row_of[None, :]
    by_row = jnp.dot(
        planes.astype(jnp.bfloat16).reshape(local_features * lat_rows, lon_cols),
        col_picker,
        preferred_element_type=jnp.bfloat16,
    ).reshape(local_features, lat_rows, cloudy)
    picked = jnp.sum(jnp.where(row_match[None], by_row, jnp.zeros_like(by_row)), axis=1)
    routes = owners[0, :, 0]
    group = lon_count * lev_count
    whole_slices = capacity == per_device
    if whole_slices:
        send_buffer = jnp.broadcast_to(
            picked.reshape(local_features, 1, lev_count, per_device),
            (local_features, lon_count, lev_count, per_device),
        ).reshape(local_features, group, capacity)
    else:
        pieces = routes.reshape(lev_count, per_device)
        onehot = (pieces[:, :, None] == jnp.arange(lon_count, dtype=jnp.int32)).astype(jnp.int32)
        slot_rank = jnp.sum(jnp.cumsum(onehot, 1) * onehot, 2) - 1
        piece_of = jnp.arange(lev_count, dtype=jnp.int32)[:, None]
        slot_index = ((pieces * lev_count + piece_of) * capacity + slot_rank).reshape(cloudy)
        send_buffer = (
            jnp.zeros((local_features, group * capacity), jnp.bfloat16)
            .at[:, slot_index]
            .set(picked)
        ).reshape(local_features, group, capacity)
    received = lax.all_to_all(
        send_buffer, ("lon", "lev"), split_axis=1, concat_axis=1, tiled=True
    )
    inputs = (
        received.reshape(2, level_rows, lon_count, lev_count, capacity)
        .transpose(0, 3, 1, 2, 4)
        .reshape(feature_count, lon_count * capacity)
    )
    outcome = network(inputs, w_in[0], w_mid[0], w_out[0])
    outgoing = (
        outcome.reshape(2, lev_count, level_rows, lon_count, capacity)
        .transpose(0, 2, 3, 1, 4)
        .reshape(local_features, group, capacity)
    )
    returned = lax.all_to_all(
        outgoing, ("lon", "lev"), split_axis=1, concat_axis=1, tiled=True
    )
    if whole_slices:
        returned = returned.reshape(local_features, lon_count, cloudy)
        tendency = returned[:, 0]
        for regime in range(1, lon_count):
            tendency = jnp.where(routes[None, :] == regime, returned[:, regime], tendency)
    else:
        tendency = returned.reshape(local_features, group * capacity)[:, slot_index]
    spread_rows = jnp.where(row_match[None], tendency[:, None, :], jnp.zeros_like(tendency)[:, None, :])
    spread = lax.dot_general(
        spread_rows.reshape(local_features * lat_rows, cloudy),
        col_picker,
        (((1,), (1,)), ((), ())),
        preferred_element_type=jnp.float32,
    )
    updated = planes + spread.reshape(planes.shape)
    return updated.reshape(values.shape)


def solution(mesh):
    in_specs = (
        P(None, "lev", "lat", "lon"),
        P("lev", "lat", "lon"),
        P("lat", "lon"),
        P("lat", "lon", None),
        P("lon", None, None),
        P("lon", None, None, None),
        P("lon", None, None),
    )
    out_specs = P(None, "lev", "lat", "lon")
    return jax.shard_map(
        on_device, mesh=mesh, in_specs=in_specs, out_specs=out_specs, check_vma=False
    )
```

```python
import jax
import jax.numpy as jnp
from jax import lax
from jax.sharding import PartitionSpec as P

LEVELS = 60
STEPS = 3


def halo_exchange(planes, diffusivity, width):
    lat_count, lon_count = lax.axis_size("lat"), lax.axis_size("lon")
    rows, cols = planes.shape[-2], planes.shape[-1]

    def both(cut):
        return jnp.concatenate([planes[cut], diffusivity[cut]], axis=0)

    from_above = lax.ppermute(
        both((slice(None), slice(rows - width, None))),
        "lat",
        [(i, i + 1) for i in range(lat_count - 1)],
    )
    from_below = lax.ppermute(
        both((slice(None), slice(0, width))), "lat", [(i + 1, i) for i in range(lat_count - 1)]
    )

    def edge(cut):
        return jnp.concatenate(
            [from_above[..., cut], both((slice(None), slice(None), cut)), from_below[..., cut]],
            axis=-2,
        )

    left, right = edge(slice(0, width)), edge(slice(cols - width, None))
    if lon_count == 2:
        swapped = lax.ppermute(jnp.concatenate([right, left], axis=-1), "lon", [(0, 1), (1, 0)])
        from_left, from_right = swapped[..., :width], swapped[..., width:]
    else:
        from_left = lax.ppermute(right, "lon", [(i, (i + 1) % lon_count) for i in range(lon_count)])
        from_right = lax.ppermute(left, "lon", [((i + 1) % lon_count, i) for i in range(lon_count)])
    stacked = jnp.concatenate([planes, diffusivity], axis=0)
    stacked = jnp.concatenate([from_above, stacked, from_below], axis=-2)
    return jnp.concatenate([from_left, stacked, from_right], axis=-1)


def substep(values, coefficients):
    centre = values[..., 1:-1, 1:-1]
    middle = coefficients[:, 1:-1, 1:-1]
    updated = centre
    for lat_cut, lon_cut in (
        (slice(0, -2), slice(1, -1)),
        (slice(2, None), slice(1, -1)),
        (slice(1, -1), slice(0, -2)),
        (slice(1, -1), slice(2, None)),
    ):
        neighbour = values[..., lat_cut, lon_cut]
        face_coef = 0.5 * (middle + coefficients[:, lat_cut, lon_cut])
        updated = updated + face_coef * (neighbour - centre)
    return updated


def clear_outside(values, rim_width, lat_rows):
    lat_pos = (
        lax.axis_index("lat") * lat_rows - rim_width + jnp.arange(values.shape[-2], dtype=jnp.int32)
    )
    inside = (lat_pos >= 0) & (lat_pos < lat_rows * lax.axis_size("lat"))
    return jnp.where(inside[:, None], values, 0.0)


def dynamics(fields, diffusivity):
    kinds, level_rows, lat_rows, lon_cols = fields.shape
    stacked = halo_exchange(
        fields.reshape(kinds * level_rows, lat_rows, lon_cols), diffusivity, STEPS
    )
    values = stacked[: kinds * level_rows].reshape(
        kinds, level_rows, lat_rows + 2 * STEPS, lon_cols + 2 * STEPS
    )
    kappa = stacked[kinds * level_rows :]
    for repeat in range(STEPS):
        trim = repeat
        coefficients = kappa[:, trim : kappa.shape[1] - trim, trim : kappa.shape[2] - trim]
        values = substep(values, coefficients)
        rim = STEPS - repeat - 1
        if rim:
            values = clear_outside(values, rim, lat_rows)
    return values


def network(features, w_first, w_middle, w_last):
    contract = (((0,), (0,)), ((), ()))
    hidden = jax.nn.gelu(
        lax.dot_general(w_first, features, contract, preferred_element_type=jnp.float32)
    ).astype(jnp.bfloat16)
    for layer_no in range(w_middle.shape[0]):
        hidden = jax.nn.gelu(
            lax.dot_general(
                w_middle[layer_no], hidden, contract, preferred_element_type=jnp.float32
            )
        ).astype(jnp.bfloat16)
    return lax.dot_general(w_last, hidden, contract, preferred_element_type=jnp.float32).astype(
        jnp.bfloat16
    )


def on_device(fields, diffusivity, cloudy_index, owners, w_in, w_mid, w_out):
    values = dynamics(fields, diffusivity)
    lev_count = lax.axis_size("lev")
    lon_count = lax.axis_size("lon")
    level_rows = values.shape[1]
    cells = values.shape[2] * values.shape[3]
    column_ids = cloudy_index[0]
    cloudy = column_ids.shape[0]
    per_device = cloudy // lev_count
    capacity = min(per_device, 4 * per_device // lon_count)
    feature_count = 2 * LEVELS
    lat_rows, lon_cols = values.shape[2], values.shape[3]
    local_features = 2 * level_rows
    planes = values.reshape(local_features, lat_rows, lon_cols)
    row_of = column_ids // lon_cols
    col_of = column_ids % lon_cols
    col_picker = (jnp.arange(lon_cols, dtype=jnp.int32)[:, None] == col_of[None, :]).astype(
        jnp.bfloat16
    )
    row_match = jnp.arange(lat_rows, dtype=jnp.int32)[:, None] == row_of[None, :]
    by_row = jnp.dot(
        planes.astype(jnp.bfloat16).reshape(local_features * lat_rows, lon_cols),
        col_picker,
        preferred_element_type=jnp.bfloat16,
    ).reshape(local_features, lat_rows, cloudy)
    picked = jnp.sum(jnp.where(row_match[None], by_row, jnp.zeros_like(by_row)), axis=1)
    routes = owners[0, :, 0]
    group = lon_count * lev_count
    whole_slices = capacity == per_device
    if whole_slices:
        send_buffer = jnp.broadcast_to(
            picked.reshape(local_features, 1, lev_count, per_device),
            (local_features, lon_count, lev_count, per_device),
        ).reshape(local_features, group, capacity)
    else:
        pieces = routes.reshape(lev_count, per_device)
        onehot = (pieces[:, :, None] == jnp.arange(lon_count, dtype=jnp.int32)).astype(jnp.int32)
        slot_rank = jnp.sum(jnp.cumsum(onehot, 1) * onehot, 2) - 1
        piece_of = jnp.arange(lev_count, dtype=jnp.int32)[:, None]
        slot_index = ((pieces * lev_count + piece_of) * capacity + slot_rank).reshape(cloudy)
        send_buffer = (
            jnp.zeros((local_features, group * capacity), jnp.bfloat16)
            .at[:, slot_index]
            .set(picked)
        ).reshape(local_features, group, capacity)
    received = lax.all_to_all(
        send_buffer, ("lon", "lev"), split_axis=1, concat_axis=1, tiled=True
    )
    inputs = (
        received.reshape(2, level_rows, lon_count, lev_count, capacity)
        .transpose(0, 3, 1, 2, 4)
        .reshape(feature_count, lon_count * capacity)
    )
    outcome = network(inputs, w_in[0], w_mid[0], w_out[0])
    outgoing = (
        outcome.reshape(2, lev_count, level_rows, lon_count, capacity)
        .transpose(0, 2, 3, 1, 4)
        .reshape(local_features, group, capacity)
    )
    returned = lax.all_to_all(
        outgoing, ("lon", "lev"), split_axis=1, concat_axis=1, tiled=True
    )
    if whole_slices:
        returned = returned.reshape(local_features, lon_count, cloudy)
        tendency = returned[:, 0]
        for regime in range(1, lon_count):
            tendency = jnp.where(routes[None, :] == regime, returned[:, regime], tendency)
    else:
        tendency = returned.reshape(local_features, group * capacity)[:, slot_index]
    spread_rows = jnp.where(row_match[None], tendency[:, None, :], jnp.zeros_like(tendency)[:, None, :])
    spread = lax.dot_general(
        spread_rows.reshape(local_features * lat_rows, cloudy),
        col_picker,
        (((1,), (1,)), ((), ())),
        preferred_element_type=jnp.float32,
    )
    updated = planes + spread.reshape(planes.shape)
    return updated.reshape(values.shape)


def solution(mesh):
    in_specs = (
        P(None, "lev", "lat", "lon"),
        P("lev", "lat", "lon"),
        P("lat", "lon"),
        P("lat", "lon", None),
        P("lon", None, None),
        P("lon", None, None, None),
        P("lon", None, None),
    )
    out_specs = P(None, "lev", "lat", "lon")
    return jax.shard_map(
        on_device, mesh=mesh, in_specs=in_specs, out_specs=out_specs, check_vma=False
    )
```

```python
import jax
import jax.numpy as jnp
from jax import lax
from jax.sharding import PartitionSpec as P

LEVELS = 60
STEPS = 3


def halo_exchange(cells, width):
    lon_count = lax.axis_size("lon")
    left = cells[..., :width]
    right = cells[..., cells.shape[-1] - width :]
    if lon_count == 2:
        both = lax.ppermute(jnp.concatenate([right, left], axis=-1), "lon", [(0, 1), (1, 0)])
        from_left, from_right = both[..., :width], both[..., width:]
    else:
        from_left = lax.ppermute(right, "lon", [(i, (i + 1) % lon_count) for i in range(lon_count)])
        from_right = lax.ppermute(left, "lon", [((i + 1) % lon_count, i) for i in range(lon_count)])
    cells = jnp.concatenate([from_left, cells, from_right], axis=-1)
    lat_count = lax.axis_size("lat")
    from_above = lax.ppermute(
        cells[..., cells.shape[-2] - width :, :], "lat", [(i, i + 1) for i in range(lat_count - 1)]
    )
    from_below = lax.ppermute(
        cells[..., :width, :], "lat", [(i + 1, i) for i in range(lat_count - 1)]
    )
    return jnp.concatenate([from_above, cells, from_below], axis=-2)


def substep(values, coefficients):
    centre = values[..., 1:-1, 1:-1]
    middle = coefficients[:, 1:-1, 1:-1]
    updated = centre
    for lat_cut, lon_cut in (
        (slice(0, -2), slice(1, -1)),
        (slice(2, None), slice(1, -1)),
        (slice(1, -1), slice(0, -2)),
        (slice(1, -1), slice(2, None)),
    ):
        neighbour = values[..., lat_cut, lon_cut]
        face_coef = 0.5 * (middle + coefficients[:, lat_cut, lon_cut])
        updated = updated + face_coef * (neighbour - centre)
    return updated


def clear_outside(values, rim_width, lat_rows):
    lat_pos = (
        lax.axis_index("lat") * lat_rows - rim_width + jnp.arange(values.shape[-2], dtype=jnp.int32)
    )
    inside = (lat_pos >= 0) & (lat_pos < lat_rows * lax.axis_size("lat"))
    return jnp.where(inside[:, None], values, 0.0)


def dynamics(fields, diffusivity):
    kinds, level_rows, lat_rows, lon_cols = fields.shape
    stacked = jnp.concatenate(
        [fields.reshape(kinds * level_rows, lat_rows, lon_cols), diffusivity], axis=0
    )
    stacked = halo_exchange(stacked, STEPS)
    values = stacked[: kinds * level_rows].reshape(
        kinds, level_rows, lat_rows + 2 * STEPS, lon_cols + 2 * STEPS
    )
    kappa = stacked[kinds * level_rows :]
    for repeat in range(STEPS):
        trim = repeat
        coefficients = kappa[:, trim : kappa.shape[1] - trim, trim : kappa.shape[2] - trim]
        values = substep(values, coefficients)
        rim = STEPS - repeat - 1
        if rim:
            values = clear_outside(values, rim, lat_rows)
    return values


def network(features, w_first, w_middle, w_last):
    contract = (((0,), (0,)), ((), ()))
    hidden = jax.nn.gelu(
        lax.dot_general(w_first, features, contract, preferred_element_type=jnp.float32)
    ).astype(jnp.bfloat16)
    for layer_no in range(w_middle.shape[0]):
        hidden = jax.nn.gelu(
            lax.dot_general(
                w_middle[layer_no], hidden, contract, preferred_element_type=jnp.float32
            )
        ).astype(jnp.bfloat16)
    return lax.dot_general(w_last, hidden, contract, preferred_element_type=jnp.float32).astype(
        jnp.bfloat16
    )


def on_device(fields, diffusivity, cloudy_index, owners, w_in, w_mid, w_out):
    values = dynamics(fields, diffusivity)
    lev_count = lax.axis_size("lev")
    lon_count = lax.axis_size("lon")
    level_rows = values.shape[1]
    cells = values.shape[2] * values.shape[3]
    column_ids = cloudy_index[0]
    cloudy = column_ids.shape[0]
    per_device = cloudy // lev_count
    capacity = min(per_device, 4 * per_device // lon_count)
    feature_count = 2 * LEVELS
    lat_rows, lon_cols = values.shape[2], values.shape[3]
    local_features = 2 * level_rows
    planes = values.reshape(local_features, lat_rows, lon_cols)
    row_of = column_ids // lon_cols
    col_of = column_ids % lon_cols
    col_picker = (jnp.arange(lon_cols, dtype=jnp.int32)[:, None] == col_of[None, :]).astype(
        jnp.bfloat16
    )
    row_match = jnp.arange(lat_rows, dtype=jnp.int32)[:, None] == row_of[None, :]
    by_row = jnp.dot(
        planes.astype(jnp.bfloat16).reshape(local_features * lat_rows, lon_cols),
        col_picker,
        preferred_element_type=jnp.bfloat16,
    ).reshape(local_features, lat_rows, cloudy)
    picked = jnp.sum(jnp.where(row_match[None], by_row, jnp.zeros_like(by_row)), axis=1)
    routes = owners[0, :, 0]
    group = lon_count * lev_count
    whole_slices = capacity == per_device
    if whole_slices:
        send_buffer = jnp.broadcast_to(
            picked.reshape(local_features, 1, lev_count, per_device),
            (local_features, lon_count, lev_count, per_device),
        ).reshape(local_features, group, capacity)
    else:
        pieces = routes.reshape(lev_count, per_device)
        onehot = (pieces[:, :, None] == jnp.arange(lon_count, dtype=jnp.int32)).astype(jnp.int32)
        slot_rank = jnp.sum(jnp.cumsum(onehot, 1) * onehot, 2) - 1
        piece_of = jnp.arange(lev_count, dtype=jnp.int32)[:, None]
        slot_index = ((pieces * lev_count + piece_of) * capacity + slot_rank).reshape(cloudy)
        send_buffer = (
            jnp.zeros((local_features, group * capacity), jnp.bfloat16)
            .at[:, slot_index]
            .set(picked)
        ).reshape(local_features, group, capacity)
    received = lax.all_to_all(
        send_buffer, ("lon", "lev"), split_axis=1, concat_axis=1, tiled=True
    )
    inputs = (
        received.reshape(2, level_rows, lon_count, lev_count, capacity)
        .transpose(0, 3, 1, 2, 4)
        .reshape(feature_count, lon_count * capacity)
    )
    outcome = network(inputs, w_in[0], w_mid[0], w_out[0])
    outgoing = (
        outcome.reshape(2, lev_count, level_rows, lon_count, capacity)
        .transpose(0, 2, 3, 1, 4)
        .reshape(local_features, group, capacity)
    )
    returned = lax.all_to_all(
        outgoing, ("lon", "lev"), split_axis=1, concat_axis=1, tiled=True
    )
    if whole_slices:
        returned = returned.reshape(local_features, lon_count, cloudy)
        tendency = returned[:, 0]
        for regime in range(1, lon_count):
            tendency = jnp.where(routes[None, :] == regime, returned[:, regime], tendency)
    else:
        tendency = returned.reshape(local_features, group * capacity)[:, slot_index]
    spread_rows = jnp.where(row_match[None], tendency[:, None, :], jnp.zeros_like(tendency)[:, None, :])
    spread = lax.dot_general(
        spread_rows.reshape(local_features * lat_rows, cloudy),
        col_picker,
        (((1,), (1,)), ((), ())),
        preferred_element_type=jnp.float32,
    )
    updated = planes + spread.reshape(planes.shape)
    return updated.reshape(values.shape)


def solution(mesh):
    in_specs = (
        P(None, "lev", "lat", "lon"),
        P("lev", "lat", "lon"),
        P("lat", "lon"),
        P("lat", "lon", None),
        P("lon", None, None),
        P("lon", None, None, None),
        P("lon", None, None),
    )
    out_specs = P(None, "lev", "lat", "lon")
    return jax.shard_map(
        on_device, mesh=mesh, in_specs=in_specs, out_specs=out_specs, check_vma=False
    )
```

```python
import jax
import jax.numpy as jnp
from jax import lax
from jax.experimental import pallas as pl
from jax.experimental.pallas import tpu as pltpu
from jax.sharding import PartitionSpec as P

LEVELS = 60
STEPS = 3


def stencil_kernel(own_ref, kappa_ref, rows_ref, lanes_ref, mask_ref, out_ref):
    kinds, levels = out_ref.shape[0], out_ref.shape[1]
    lat_rows, lon_cols = out_ref.shape[2], out_ref.shape[3]
    mask = mask_ref[...] > 0.5
    tile_rows = lat_rows + rows_ref.shape[1]
    tile_cols = lon_cols + lanes_ref.shape[2]
    shifts = ((1, 0), (tile_rows - 1, 0), (1, 1), (tile_cols - 1, 1))

    def tile(own, plane):
        top = jnp.concatenate([own, rows_ref[plane]], axis=0)
        return jnp.concatenate([top, lanes_ref[plane]], axis=1)

    def level(index, carry):
        kappa = tile(kappa_ref[index], kinds * levels + index)
        faces = [0.5 * (kappa + pltpu.roll(kappa, shift, axis)) for shift, axis in shifts]
        for kind in range(kinds):
            plane = kind * levels + index
            values = tile(own_ref[plane], plane)
            for repeat in range(STEPS):
                updated = values
                for face, (shift, axis) in zip(faces, shifts):
                    updated = updated + face * (pltpu.roll(values, shift, axis) - values)
                values = jnp.where(mask, updated, 0.0)
            out_ref[kind, index] = values[:lat_rows, :lon_cols]
        return carry

    lax.fori_loop(0, levels, level, 0)


def dynamics(fields, diffusivity):
    kinds, level_rows, lat_rows, lon_cols = fields.shape
    planes = fields.reshape(kinds * level_rows, lat_rows, lon_cols)
    lat_count, lon_count = lax.axis_size("lat"), lax.axis_size("lon")
    width = STEPS
    row_pad = 8 * ((2 * width + 7) // 8)
    lane_pad = 128 * ((2 * width + 127) // 128)

    def both(cut):
        return jnp.concatenate([planes[cut], diffusivity[cut]], axis=0)

    north = lax.ppermute(
        both((slice(None), slice(lat_rows - width, None))),
        "lat",
        [(i, i + 1) for i in range(lat_count - 1)],
    )
    south = lax.ppermute(
        both((slice(None), slice(0, width))), "lat", [(i + 1, i) for i in range(lat_count - 1)]
    )
    gap = jnp.zeros((north.shape[0], row_pad - 2 * width, lon_cols), north.dtype)
    row_block = jnp.concatenate([south, gap, north], axis=1)

    def edge(cut):
        return jnp.concatenate(
            [both((slice(None), slice(None), cut)), row_block[..., cut]], axis=1
        )

    left, right = edge(slice(0, width)), edge(slice(lon_cols - width, None))
    if lon_count == 2:
        swapped = lax.ppermute(jnp.concatenate([right, left], axis=-1), "lon", [(0, 1), (1, 0)])
        west, east = swapped[..., :width], swapped[..., width:]
    else:
        west = lax.ppermute(right, "lon", [(i, (i + 1) % lon_count) for i in range(lon_count)])
        east = lax.ppermute(left, "lon", [((i + 1) % lon_count, i) for i in range(lon_count)])
    lane_gap = jnp.zeros(east.shape[:2] + (lane_pad - 2 * width,), east.dtype)
    lane_block = jnp.concatenate([east, lane_gap, west], axis=-1)
    tile_rows = lat_rows + row_pad
    row_ids = jnp.arange(tile_rows, dtype=jnp.int32)
    offset = jnp.where(row_ids < lat_rows + row_pad - width, row_ids, row_ids - tile_rows)
    global_row = lax.axis_index("lat") * lat_rows + offset
    inside = (global_row >= 0) & (global_row < lat_rows * lat_count)
    mask = jnp.broadcast_to(inside[:, None], (tile_rows, lon_cols + lane_pad)).astype(jnp.float32)
    vmem = pl.BlockSpec(memory_space=pltpu.VMEM)
    cells = kinds * level_rows * lat_rows * lon_cols
    return pl.pallas_call(
        stencil_kernel,
        out_shape=jax.ShapeDtypeStruct(fields.shape, fields.dtype),
        in_specs=[vmem] * 5,
        out_specs=vmem,
        cost_estimate=pl.CostEstimate(
            flops=60 * cells, transcendentals=0, bytes_accessed=16 * cells
        ),
    )(planes, diffusivity, row_block, lane_block, mask)


def network(features, w_first, w_middle, w_last):
    contract = (((0,), (0,)), ((), ()))
    hidden = jax.nn.gelu(
        lax.dot_general(w_first, features, contract, preferred_element_type=jnp.float32)
    ).astype(jnp.bfloat16)
    for layer_no in range(w_middle.shape[0]):
        hidden = jax.nn.gelu(
            lax.dot_general(
                w_middle[layer_no], hidden, contract, preferred_element_type=jnp.float32
            )
        ).astype(jnp.bfloat16)
    return lax.dot_general(w_last, hidden, contract, preferred_element_type=jnp.float32).astype(
        jnp.bfloat16
    )


def on_device(fields, diffusivity, cloudy_index, owners, w_in, w_mid, w_out):
    values = dynamics(fields, diffusivity)
    lev_count = lax.axis_size("lev")
    lon_count = lax.axis_size("lon")
    level_rows = values.shape[1]
    cells = values.shape[2] * values.shape[3]
    column_ids = cloudy_index[0]
    cloudy = column_ids.shape[0]
    per_device = cloudy // lev_count
    capacity = min(per_device, 4 * per_device // lon_count)
    feature_count = 2 * LEVELS
    lat_rows, lon_cols = values.shape[2], values.shape[3]
    local_features = 2 * level_rows
    planes = values.reshape(local_features, lat_rows, lon_cols)
    row_of = column_ids // lon_cols
    col_of = column_ids % lon_cols
    col_picker = (jnp.arange(lon_cols, dtype=jnp.int32)[:, None] == col_of[None, :]).astype(
        jnp.bfloat16
    )
    row_match = jnp.arange(lat_rows, dtype=jnp.int32)[:, None] == row_of[None, :]
    by_row = jnp.dot(
        planes.astype(jnp.bfloat16).reshape(local_features * lat_rows, lon_cols),
        col_picker,
        preferred_element_type=jnp.bfloat16,
    ).reshape(local_features, lat_rows, cloudy)
    picked = jnp.sum(jnp.where(row_match[None], by_row, jnp.zeros_like(by_row)), axis=1)
    routes = owners[0, :, 0]
    group = lon_count * lev_count
    whole_slices = capacity == per_device
    if whole_slices:
        send_buffer = jnp.broadcast_to(
            picked.reshape(local_features, 1, lev_count, per_device),
            (local_features, lon_count, lev_count, per_device),
        ).reshape(local_features, group, capacity)
    else:
        pieces = routes.reshape(lev_count, per_device)
        onehot = (pieces[:, :, None] == jnp.arange(lon_count, dtype=jnp.int32)).astype(jnp.int32)
        slot_rank = jnp.sum(jnp.cumsum(onehot, 1) * onehot, 2) - 1
        piece_of = jnp.arange(lev_count, dtype=jnp.int32)[:, None]
        slot_index = ((pieces * lev_count + piece_of) * capacity + slot_rank).reshape(cloudy)
        send_buffer = (
            jnp.zeros((local_features, group * capacity), jnp.bfloat16)
            .at[:, slot_index]
            .set(picked)
        ).reshape(local_features, group, capacity)
    received = lax.all_to_all(
        send_buffer, ("lon", "lev"), split_axis=1, concat_axis=1, tiled=True
    )
    inputs = (
        received.reshape(2, level_rows, lon_count, lev_count, capacity)
        .transpose(0, 3, 1, 2, 4)
        .reshape(feature_count, lon_count * capacity)
    )
    outcome = network(inputs, w_in[0], w_mid[0], w_out[0])
    outgoing = (
        outcome.reshape(2, lev_count, level_rows, lon_count, capacity)
        .transpose(0, 2, 3, 1, 4)
        .reshape(local_features, group, capacity)
    )
    returned = lax.all_to_all(
        outgoing, ("lon", "lev"), split_axis=1, concat_axis=1, tiled=True
    )
    if whole_slices:
        returned = returned.reshape(local_features, lon_count, cloudy)
        tendency = returned[:, 0]
        for regime in range(1, lon_count):
            tendency = jnp.where(routes[None, :] == regime, returned[:, regime], tendency)
    else:
        tendency = returned.reshape(local_features, group * capacity)[:, slot_index]
    spread_rows = jnp.where(row_match[None], tendency[:, None, :], jnp.zeros_like(tendency)[:, None, :])
    spread = lax.dot_general(
        spread_rows.reshape(local_features * lat_rows, cloudy),
        col_picker,
        (((1,), (1,)), ((), ())),
        preferred_element_type=jnp.float32,
    )
    updated = planes + spread.reshape(planes.shape)
    return updated.reshape(values.shape)


def solution(mesh):
    in_specs = (
        P(None, "lev", "lat", "lon"),
        P("lev", "lat", "lon"),
        P("lat", "lon"),
        P("lat", "lon", None),
        P("lon", None, None),
        P("lon", None, None, None),
        P("lon", None, None),
    )
    out_specs = P(None, "lev", "lat", "lon")
    return jax.shard_map(
        on_device, mesh=mesh, in_specs=in_specs, out_specs=out_specs, check_vma=False
    )
```

```python
import jax
import jax.numpy as jnp
from jax import lax
from jax.sharding import PartitionSpec as P

LEVELS = 60
STEPS = 3


def halo_exchange(cells, width):
    lat_count = lax.axis_size("lat")
    from_above = lax.ppermute(
        cells[..., cells.shape[-2] - width :, :], "lat", [(i, i + 1) for i in range(lat_count - 1)]
    )
    from_below = lax.ppermute(
        cells[..., :width, :], "lat", [(i + 1, i) for i in range(lat_count - 1)]
    )
    cells = jnp.concatenate([from_above, cells, from_below], axis=-2)
    lon_count = lax.axis_size("lon")
    left = cells[..., :width]
    right = cells[..., cells.shape[-1] - width :]
    if lon_count == 2:
        both = lax.ppermute(jnp.concatenate([right, left], axis=-1), "lon", [(0, 1), (1, 0)])
        from_left, from_right = both[..., :width], both[..., width:]
    else:
        from_left = lax.ppermute(right, "lon", [(i, (i + 1) % lon_count) for i in range(lon_count)])
        from_right = lax.ppermute(left, "lon", [((i + 1) % lon_count, i) for i in range(lon_count)])
    return jnp.concatenate([from_left, cells, from_right], axis=-1)


def substep(values, coefficients):
    centre = values[..., 1:-1, 1:-1]
    middle = coefficients[:, 1:-1, 1:-1]
    updated = centre
    for lat_cut, lon_cut in (
        (slice(0, -2), slice(1, -1)),
        (slice(2, None), slice(1, -1)),
        (slice(1, -1), slice(0, -2)),
        (slice(1, -1), slice(2, None)),
    ):
        neighbour = values[..., lat_cut, lon_cut]
        face_coef = 0.5 * (middle + coefficients[:, lat_cut, lon_cut])
        updated = updated + face_coef * (neighbour - centre)
    return updated


def clear_outside(values, rim_width, lat_rows):
    lat_pos = (
        lax.axis_index("lat") * lat_rows - rim_width + jnp.arange(values.shape[-2], dtype=jnp.int32)
    )
    inside = (lat_pos >= 0) & (lat_pos < lat_rows * lax.axis_size("lat"))
    return jnp.where(inside[:, None], values, 0.0)


def dynamics(fields, diffusivity):
    kinds, level_rows, lat_rows, lon_cols = fields.shape
    stacked = jnp.concatenate(
        [fields.reshape(kinds * level_rows, lat_rows, lon_cols), diffusivity], axis=0
    )
    stacked = halo_exchange(stacked, STEPS)
    values = stacked[: kinds * level_rows].reshape(
        kinds, level_rows, lat_rows + 2 * STEPS, lon_cols + 2 * STEPS
    )
    kappa = stacked[kinds * level_rows :]
    for repeat in range(STEPS):
        trim = repeat
        coefficients = kappa[:, trim : kappa.shape[1] - trim, trim : kappa.shape[2] - trim]
        values = substep(values, coefficients)
        rim = STEPS - repeat - 1
        if rim:
            values = clear_outside(values, rim, lat_rows)
    return values


def network(features, w_first, w_middle, w_last):
    contract = (((0,), (0,)), ((), ()))
    hidden = jax.nn.gelu(
        lax.dot_general(w_first, features, contract, preferred_element_type=jnp.float32)
    ).astype(jnp.bfloat16)
    for layer_no in range(w_middle.shape[0]):
        hidden = jax.nn.gelu(
            lax.dot_general(
                w_middle[layer_no], hidden, contract, preferred_element_type=jnp.float32
            )
        ).astype(jnp.bfloat16)
    return lax.dot_general(w_last, hidden, contract, preferred_element_type=jnp.float32).astype(
        jnp.bfloat16
    )


def on_device(fields, diffusivity, cloudy_index, owners, w_in, w_mid, w_out):
    values = dynamics(fields, diffusivity)
    lev_count = lax.axis_size("lev")
    lon_count = lax.axis_size("lon")
    level_rows = values.shape[1]
    cells = values.shape[2] * values.shape[3]
    column_ids = cloudy_index[0]
    cloudy = column_ids.shape[0]
    per_device = cloudy // lev_count
    capacity = min(per_device, 4 * per_device // lon_count)
    feature_count = 2 * LEVELS
    lat_rows, lon_cols = values.shape[2], values.shape[3]
    local_features = 2 * level_rows
    planes = values.reshape(local_features, lat_rows, lon_cols)
    row_of = column_ids // lon_cols
    col_of = column_ids % lon_cols
    col_picker = (jnp.arange(lon_cols, dtype=jnp.int32)[:, None] == col_of[None, :]).astype(
        jnp.bfloat16
    )
    row_match = jnp.arange(lat_rows, dtype=jnp.int32)[:, None] == row_of[None, :]
    by_row = jnp.dot(
        planes.astype(jnp.bfloat16).reshape(local_features * lat_rows, lon_cols),
        col_picker,
        preferred_element_type=jnp.bfloat16,
    ).reshape(local_features, lat_rows, cloudy)
    picked = jnp.sum(jnp.where(row_match[None], by_row, jnp.zeros_like(by_row)), axis=1)
    routes = owners[0, :, 0]
    group = lon_count * lev_count
    whole_slices = capacity == per_device
    if whole_slices:
        send_buffer = jnp.broadcast_to(
            picked.reshape(local_features, 1, lev_count, per_device),
            (local_features, lon_count, lev_count, per_device),
        ).reshape(local_features, group, capacity)
    else:
        pieces = routes.reshape(lev_count, per_device)
        onehot = (pieces[:, :, None] == jnp.arange(lon_count, dtype=jnp.int32)).astype(jnp.int32)
        slot_rank = jnp.sum(jnp.cumsum(onehot, 1) * onehot, 2) - 1
        piece_of = jnp.arange(lev_count, dtype=jnp.int32)[:, None]
        slot_index = ((pieces * lev_count + piece_of) * capacity + slot_rank).reshape(cloudy)
        send_buffer = (
            jnp.zeros((local_features, group * capacity), jnp.bfloat16)
            .at[:, slot_index]
            .set(picked)
        ).reshape(local_features, group, capacity)
    send_buffer, late_routes, unit = lax.optimization_barrier(
        (send_buffer, routes, jnp.ones((), w_in.dtype))
    )
    first_layer = lax.optimization_barrier(w_in[0] * unit)
    received = lax.all_to_all(
        send_buffer, ("lon", "lev"), split_axis=1, concat_axis=1, tiled=True
    )
    owned = [late_routes[None, :] == regime for regime in range(lon_count)]
    inputs = (
        received.reshape(2, level_rows, lon_count, lev_count, capacity)
        .transpose(0, 3, 1, 2, 4)
        .reshape(feature_count, lon_count * capacity)
    )
    outcome = network(inputs, first_layer, w_mid[0], w_out[0])
    outgoing = (
        outcome.reshape(2, lev_count, level_rows, lon_count, capacity)
        .transpose(0, 2, 3, 1, 4)
        .reshape(local_features, group, capacity)
    )
    returned = lax.all_to_all(
        outgoing, ("lon", "lev"), split_axis=1, concat_axis=1, tiled=True
    )
    if whole_slices:
        returned = returned.reshape(local_features, lon_count, cloudy)
        tendency = returned[:, 0]
        for regime in range(1, lon_count):
            tendency = jnp.where(owned[regime], returned[:, regime], tendency)
    else:
        tendency = returned.reshape(local_features, group * capacity)[:, slot_index]
    spread_rows = jnp.where(row_match[None], tendency[:, None, :], jnp.zeros_like(tendency)[:, None, :])
    spread = lax.dot_general(
        spread_rows.reshape(local_features * lat_rows, cloudy),
        col_picker,
        (((1,), (1,)), ((), ())),
        preferred_element_type=jnp.float32,
    )
    updated = planes + spread.reshape(planes.shape)
    return updated.reshape(values.shape)


def solution(mesh):
    in_specs = (
        P(None, "lev", "lat", "lon"),
        P("lev", "lat", "lon"),
        P("lat", "lon"),
        P("lat", "lon", None),
        P("lon", None, None),
        P("lon", None, None, None),
        P("lon", None, None),
    )
    out_specs = P(None, "lev", "lat", "lon")
    return jax.shard_map(
        on_device, mesh=mesh, in_specs=in_specs, out_specs=out_specs, check_vma=False
    )
```

```python
import jax
import jax.numpy as jnp
from jax import lax
from jax.experimental import pallas as pl
from jax.experimental.pallas import tpu as pltpu
from jax.sharding import PartitionSpec as P

LEVELS = 60
STEPS = 3


def halo_exchange(cells, width):
    lat_count = lax.axis_size("lat")
    from_above = lax.ppermute(
        cells[..., cells.shape[-2] - width :, :], "lat", [(i, i + 1) for i in range(lat_count - 1)]
    )
    from_below = lax.ppermute(
        cells[..., :width, :], "lat", [(i + 1, i) for i in range(lat_count - 1)]
    )
    cells = jnp.concatenate([from_above, cells, from_below], axis=-2)
    lon_count = lax.axis_size("lon")
    left = cells[..., :width]
    right = cells[..., cells.shape[-1] - width :]
    if lon_count == 2:
        both = lax.ppermute(jnp.concatenate([right, left], axis=-1), "lon", [(0, 1), (1, 0)])
        from_left, from_right = both[..., :width], both[..., width:]
    else:
        from_left = lax.ppermute(right, "lon", [(i, (i + 1) % lon_count) for i in range(lon_count)])
        from_right = lax.ppermute(left, "lon", [((i + 1) % lon_count, i) for i in range(lon_count)])
    return jnp.concatenate([from_left, cells, from_right], axis=-1)


def substep(values, coefficients):
    centre = values[..., 1:-1, 1:-1]
    middle = coefficients[:, 1:-1, 1:-1]
    updated = centre
    for lat_cut, lon_cut in (
        (slice(0, -2), slice(1, -1)),
        (slice(2, None), slice(1, -1)),
        (slice(1, -1), slice(0, -2)),
        (slice(1, -1), slice(2, None)),
    ):
        neighbour = values[..., lat_cut, lon_cut]
        face_coef = 0.5 * (middle + coefficients[:, lat_cut, lon_cut])
        updated = updated + face_coef * (neighbour - centre)
    return updated


def clear_outside(values, rim_width, lat_rows):
    lat_pos = (
        lax.axis_index("lat") * lat_rows - rim_width + jnp.arange(values.shape[-2], dtype=jnp.int32)
    )
    inside = (lat_pos >= 0) & (lat_pos < lat_rows * lax.axis_size("lat"))
    return jnp.where(inside[:, None], values, 0.0)


def dynamics(fields, diffusivity):
    kinds, level_rows, lat_rows, lon_cols = fields.shape
    stacked = jnp.concatenate(
        [fields.reshape(kinds * level_rows, lat_rows, lon_cols), diffusivity], axis=0
    )
    stacked = halo_exchange(stacked, STEPS)
    values = stacked[: kinds * level_rows].reshape(
        kinds, level_rows, lat_rows + 2 * STEPS, lon_cols + 2 * STEPS
    )
    kappa = stacked[kinds * level_rows :]
    for repeat in range(STEPS):
        trim = repeat
        coefficients = kappa[:, trim : kappa.shape[1] - trim, trim : kappa.shape[2] - trim]
        values = substep(values, coefficients)
        rim = STEPS - repeat - 1
        if rim:
            values = clear_outside(values, rim, lat_rows)
    return values


def network_kernel(rows_ref, first_ref, middle_ref, last_ref, out_ref):
    tile = min(rows_ref.shape[0], 512)

    def one_tile(index, carry):
        rows = pl.ds(pl.multiple_of(index * tile, tile), tile)
        hidden = jax.nn.gelu(
            jnp.dot(rows_ref[rows, :], first_ref[...], preferred_element_type=jnp.float32)
        ).astype(jnp.bfloat16)
        for layer_no in range(middle_ref.shape[0]):
            hidden = jax.nn.gelu(
                jnp.dot(hidden, middle_ref[layer_no], preferred_element_type=jnp.float32)
            ).astype(jnp.bfloat16)
        out_ref[rows, :] = jnp.dot(
            hidden, last_ref[...], preferred_element_type=jnp.float32
        ).astype(jnp.bfloat16)
        return carry

    lax.fori_loop(0, rows_ref.shape[0] // tile, one_tile, 0)


def network(rows, w_first, w_middle, w_last):
    count, width = rows.shape
    hid = w_first.shape[1]
    vmem = pl.BlockSpec(memory_space=pltpu.VMEM)
    flops = 2 * count * (width * hid + w_middle.shape[0] * hid * hid + hid * w_last.shape[1])
    weight_bytes = 2 * (w_first.size + w_middle.size + w_last.size)
    return pl.pallas_call(
        network_kernel,
        out_shape=jax.ShapeDtypeStruct((count, w_last.shape[1]), jnp.bfloat16),
        in_specs=[vmem] * 4,
        out_specs=vmem,
        compiler_params=pltpu.CompilerParams(vmem_limit_bytes=48 * 1024 * 1024),
        cost_estimate=pl.CostEstimate(
            flops=flops,
            transcendentals=(1 + w_middle.shape[0]) * count * hid,
            bytes_accessed=weight_bytes + 2 * count * (width + w_last.shape[1]),
        ),
    )(rows, w_first, w_middle, w_last)


def on_device(fields, diffusivity, cloudy_index, owners, w_in, w_mid, w_out):
    values = dynamics(fields, diffusivity)
    lev_count = lax.axis_size("lev")
    lon_count = lax.axis_size("lon")
    level_rows = values.shape[1]
    cells = values.shape[2] * values.shape[3]
    column_ids = cloudy_index[0]
    cloudy = column_ids.shape[0]
    per_device = cloudy // lev_count
    capacity = min(per_device, 4 * per_device // lon_count)
    feature_count = 2 * LEVELS
    lat_rows, lon_cols = values.shape[2], values.shape[3]
    local_features = 2 * level_rows
    planes = values.reshape(local_features, lat_rows, lon_cols)
    row_of = column_ids // lon_cols
    col_of = column_ids % lon_cols
    col_picker = (jnp.arange(lon_cols, dtype=jnp.int32)[:, None] == col_of[None, :]).astype(
        jnp.bfloat16
    )
    row_match = jnp.arange(lat_rows, dtype=jnp.int32)[:, None] == row_of[None, :]
    by_row = jnp.dot(
        planes.astype(jnp.bfloat16).reshape(local_features * lat_rows, lon_cols),
        col_picker,
        preferred_element_type=jnp.bfloat16,
    ).reshape(local_features, lat_rows, cloudy)
    picked = jnp.sum(jnp.where(row_match[None], by_row, jnp.zeros_like(by_row)), axis=1)
    routes = owners[0, :, 0]
    group = lon_count * lev_count
    whole_slices = capacity == per_device
    if whole_slices:
        send_buffer = jnp.broadcast_to(
            picked.reshape(local_features, 1, lev_count, per_device),
            (local_features, lon_count, lev_count, per_device),
        ).reshape(local_features, group, capacity)
    else:
        pieces = routes.reshape(lev_count, per_device)
        onehot = (pieces[:, :, None] == jnp.arange(lon_count, dtype=jnp.int32)).astype(jnp.int32)
        slot_rank = jnp.sum(jnp.cumsum(onehot, 1) * onehot, 2) - 1
        piece_of = jnp.arange(lev_count, dtype=jnp.int32)[:, None]
        slot_index = ((pieces * lev_count + piece_of) * capacity + slot_rank).reshape(cloudy)
        send_buffer = (
            jnp.zeros((local_features, group * capacity), jnp.bfloat16)
            .at[:, slot_index]
            .set(picked)
        ).reshape(local_features, group, capacity)
    received = lax.all_to_all(
        send_buffer, ("lon", "lev"), split_axis=1, concat_axis=1, tiled=True
    )
    inputs = (
        received.reshape(2, level_rows, lon_count, lev_count, capacity)
        .transpose(2, 4, 0, 3, 1)
        .reshape(lon_count * capacity, feature_count)
    )
    outcome = network(inputs, w_in[0], w_mid[0], w_out[0])
    outgoing = (
        outcome.reshape(lon_count, capacity, 2, lev_count, level_rows)
        .transpose(2, 4, 0, 3, 1)
        .reshape(local_features, group, capacity)
    )
    returned = lax.all_to_all(
        outgoing, ("lon", "lev"), split_axis=1, concat_axis=1, tiled=True
    )
    if whole_slices:
        returned = returned.reshape(local_features, lon_count, cloudy)
        tendency = returned[:, 0]
        for regime in range(1, lon_count):
            tendency = jnp.where(routes[None, :] == regime, returned[:, regime], tendency)
    else:
        tendency = returned.reshape(local_features, group * capacity)[:, slot_index]
    spread_rows = jnp.where(row_match[None], tendency[:, None, :], jnp.zeros_like(tendency)[:, None, :])
    spread = lax.dot_general(
        spread_rows.reshape(local_features * lat_rows, cloudy),
        col_picker,
        (((1,), (1,)), ((), ())),
        preferred_element_type=jnp.float32,
    )
    updated = planes + spread.reshape(planes.shape)
    return updated.reshape(values.shape)


def solution(mesh):
    in_specs = (
        P(None, "lev", "lat", "lon"),
        P("lev", "lat", "lon"),
        P("lat", "lon"),
        P("lat", "lon", None),
        P("lon", None, None),
        P("lon", None, None, None),
        P("lon", None, None),
    )
    out_specs = P(None, "lev", "lat", "lon")
    return jax.shard_map(
        on_device, mesh=mesh, in_specs=in_specs, out_specs=out_specs, check_vma=False
    )
```

```python
import functools

import jax
import jax.numpy as jnp
from jax import lax
from jax.experimental import pallas as pl
from jax.experimental.pallas import tpu as pltpu
from jax.sharding import PartitionSpec as P

LEVELS = 60
STEPS = 3


def halo_exchange(cells, width):
    lat_count = lax.axis_size("lat")
    from_above = lax.ppermute(
        cells[..., cells.shape[-2] - width :, :], "lat", [(i, i + 1) for i in range(lat_count - 1)]
    )
    from_below = lax.ppermute(
        cells[..., :width, :], "lat", [(i + 1, i) for i in range(lat_count - 1)]
    )
    cells = jnp.concatenate([from_above, cells, from_below], axis=-2)
    lon_count = lax.axis_size("lon")
    left = cells[..., :width]
    right = cells[..., cells.shape[-1] - width :]
    if lon_count == 2:
        both = lax.ppermute(jnp.concatenate([right, left], axis=-1), "lon", [(0, 1), (1, 0)])
        from_left, from_right = both[..., :width], both[..., width:]
    else:
        from_left = lax.ppermute(right, "lon", [(i, (i + 1) % lon_count) for i in range(lon_count)])
        from_right = lax.ppermute(left, "lon", [((i + 1) % lon_count, i) for i in range(lon_count)])
    return jnp.concatenate([from_left, cells, from_right], axis=-1)


def substep(values, coefficients):
    centre = values[..., 1:-1, 1:-1]
    middle = coefficients[:, 1:-1, 1:-1]
    updated = centre
    for lat_cut, lon_cut in (
        (slice(0, -2), slice(1, -1)),
        (slice(2, None), slice(1, -1)),
        (slice(1, -1), slice(0, -2)),
        (slice(1, -1), slice(2, None)),
    ):
        neighbour = values[..., lat_cut, lon_cut]
        face_coef = 0.5 * (middle + coefficients[:, lat_cut, lon_cut])
        updated = updated + face_coef * (neighbour - centre)
    return updated


def clear_outside(values, rim_width, lat_rows):
    lat_pos = (
        lax.axis_index("lat") * lat_rows - rim_width + jnp.arange(values.shape[-2], dtype=jnp.int32)
    )
    inside = (lat_pos >= 0) & (lat_pos < lat_rows * lax.axis_size("lat"))
    return jnp.where(inside[:, None], values, 0.0)


def dynamics(fields, diffusivity):
    kinds, level_rows, lat_rows, lon_cols = fields.shape
    stacked = jnp.concatenate(
        [fields.reshape(kinds * level_rows, lat_rows, lon_cols), diffusivity], axis=0
    )
    stacked = halo_exchange(stacked, STEPS)
    values = stacked[: kinds * level_rows].reshape(
        kinds, level_rows, lat_rows + 2 * STEPS, lon_cols + 2 * STEPS
    )
    kappa = stacked[kinds * level_rows :]
    for repeat in range(STEPS):
        trim = repeat
        coefficients = kappa[:, trim : kappa.shape[1] - trim, trim : kappa.shape[2] - trim]
        values = substep(values, coefficients)
        rim = STEPS - repeat - 1
        if rim:
            values = clear_outside(values, rim, lat_rows)
    return values


def layers_kernel(rows_ref, *refs, finals):
    out_ref = refs[-1]
    hidden = rows_ref[...]
    for number, weight_ref in enumerate(refs[:-1]):
        hidden = jnp.dot(hidden, weight_ref[...], preferred_element_type=jnp.float32)
        if number < len(refs) - 2 or not finals:
            hidden = jax.nn.gelu(hidden)
        hidden = hidden.astype(jnp.bfloat16)
    out_ref[...] = hidden


def layers(rows, weights, finals):
    count = rows.shape[0]
    vmem = pl.BlockSpec(memory_space=pltpu.VMEM)
    flops = sum(2 * count * w.shape[0] * w.shape[1] for w in weights)
    return pl.pallas_call(
        functools.partial(layers_kernel, finals=finals),
        out_shape=jax.ShapeDtypeStruct((count, weights[-1].shape[1]), jnp.bfloat16),
        in_specs=[vmem] * (1 + len(weights)),
        out_specs=vmem,
        compiler_params=pltpu.CompilerParams(vmem_limit_bytes=48 * 1024 * 1024),
        cost_estimate=pl.CostEstimate(
            flops=flops,
            transcendentals=count * sum(w.shape[1] for w in weights),
            bytes_accessed=sum(2 * w.size for w in weights) + 2 * count * (rows.shape[1] + weights[-1].shape[1]),
        ),
    )(rows, *weights)


def network(rows, w_first, w_middle, w_last):
    hidden = layers(rows, [w_first, w_middle[0]], finals=False)
    return layers(hidden, [w_middle[layer_no] for layer_no in range(1, w_middle.shape[0])] + [w_last], finals=True)


def on_device(fields, diffusivity, cloudy_index, owners, w_in, w_mid, w_out):
    values = dynamics(fields, diffusivity)
    lev_count = lax.axis_size("lev")
    lon_count = lax.axis_size("lon")
    level_rows = values.shape[1]
    cells = values.shape[2] * values.shape[3]
    column_ids = cloudy_index[0]
    cloudy = column_ids.shape[0]
    per_device = cloudy // lev_count
    capacity = min(per_device, 4 * per_device // lon_count)
    feature_count = 2 * LEVELS
    lat_rows, lon_cols = values.shape[2], values.shape[3]
    local_features = 2 * level_rows
    planes = values.reshape(local_features, lat_rows, lon_cols)
    row_of = column_ids // lon_cols
    col_of = column_ids % lon_cols
    col_picker = (jnp.arange(lon_cols, dtype=jnp.int32)[:, None] == col_of[None, :]).astype(
        jnp.bfloat16
    )
    row_match = jnp.arange(lat_rows, dtype=jnp.int32)[:, None] == row_of[None, :]
    by_row = jnp.dot(
        planes.astype(jnp.bfloat16).reshape(local_features * lat_rows, lon_cols),
        col_picker,
        preferred_element_type=jnp.bfloat16,
    ).reshape(local_features, lat_rows, cloudy)
    picked = jnp.sum(jnp.where(row_match[None], by_row, jnp.zeros_like(by_row)), axis=1)
    routes = owners[0, :, 0]
    group = lon_count * lev_count
    whole_slices = capacity == per_device
    if whole_slices:
        send_buffer = jnp.broadcast_to(
            picked.reshape(local_features, 1, lev_count, per_device),
            (local_features, lon_count, lev_count, per_device),
        ).reshape(local_features, group, capacity)
    else:
        pieces = routes.reshape(lev_count, per_device)
        onehot = (pieces[:, :, None] == jnp.arange(lon_count, dtype=jnp.int32)).astype(jnp.int32)
        slot_rank = jnp.sum(jnp.cumsum(onehot, 1) * onehot, 2) - 1
        piece_of = jnp.arange(lev_count, dtype=jnp.int32)[:, None]
        slot_index = ((pieces * lev_count + piece_of) * capacity + slot_rank).reshape(cloudy)
        send_buffer = (
            jnp.zeros((local_features, group * capacity), jnp.bfloat16)
            .at[:, slot_index]
            .set(picked)
        ).reshape(local_features, group, capacity)
    received = lax.all_to_all(
        send_buffer, ("lon", "lev"), split_axis=1, concat_axis=1, tiled=True
    )
    inputs = (
        received.reshape(2, level_rows, lon_count, lev_count, capacity)
        .transpose(2, 4, 0, 3, 1)
        .reshape(lon_count * capacity, feature_count)
    )
    outcome = network(inputs, w_in[0], w_mid[0], w_out[0])
    outgoing = (
        outcome.reshape(lon_count, capacity, 2, lev_count, level_rows)
        .transpose(2, 4, 0, 3, 1)
        .reshape(local_features, group, capacity)
    )
    returned = lax.all_to_all(
        outgoing, ("lon", "lev"), split_axis=1, concat_axis=1, tiled=True
    )
    if whole_slices:
        returned = returned.reshape(local_features, lon_count, cloudy)
        tendency = returned[:, 0]
        for regime in range(1, lon_count):
            tendency = jnp.where(routes[None, :] == regime, returned[:, regime], tendency)
    else:
        tendency = returned.reshape(local_features, group * capacity)[:, slot_index]
    spread_rows = jnp.where(row_match[None], tendency[:, None, :], jnp.zeros_like(tendency)[:, None, :])
    spread = lax.dot_general(
        spread_rows.reshape(local_features * lat_rows, cloudy),
        col_picker,
        (((1,), (1,)), ((), ())),
        preferred_element_type=jnp.float32,
    )
    updated = planes + spread.reshape(planes.shape)
    return updated.reshape(values.shape)


def solution(mesh):
    in_specs = (
        P(None, "lev", "lat", "lon"),
        P("lev", "lat", "lon"),
        P("lat", "lon"),
        P("lat", "lon", None),
        P("lon", None, None),
        P("lon", None, None, None),
        P("lon", None, None),
    )
    out_specs = P(None, "lev", "lat", "lon")
    return jax.shard_map(
        on_device, mesh=mesh, in_specs=in_specs, out_specs=out_specs, check_vma=False
    )
```

```python
import jax
import jax.numpy as jnp
from jax import lax
from jax.experimental import pallas as pl
from jax.experimental.pallas import tpu as pltpu
from jax.sharding import PartitionSpec as P

LEVELS = 60
STEPS = 3


def halo_exchange(cells, width):
    lat_count = lax.axis_size("lat")
    from_above = lax.ppermute(
        cells[..., cells.shape[-2] - width :, :], "lat", [(i, i + 1) for i in range(lat_count - 1)]
    )
    from_below = lax.ppermute(
        cells[..., :width, :], "lat", [(i + 1, i) for i in range(lat_count - 1)]
    )
    cells = jnp.concatenate([from_above, cells, from_below], axis=-2)
    lon_count = lax.axis_size("lon")
    left = cells[..., :width]
    right = cells[..., cells.shape[-1] - width :]
    if lon_count == 2:
        both = lax.ppermute(jnp.concatenate([right, left], axis=-1), "lon", [(0, 1), (1, 0)])
        from_left, from_right = both[..., :width], both[..., width:]
    else:
        from_left = lax.ppermute(right, "lon", [(i, (i + 1) % lon_count) for i in range(lon_count)])
        from_right = lax.ppermute(left, "lon", [((i + 1) % lon_count, i) for i in range(lon_count)])
    return jnp.concatenate([from_left, cells, from_right], axis=-1)


def substep(values, coefficients):
    centre = values[..., 1:-1, 1:-1]
    middle = coefficients[:, 1:-1, 1:-1]
    updated = centre
    for lat_cut, lon_cut in (
        (slice(0, -2), slice(1, -1)),
        (slice(2, None), slice(1, -1)),
        (slice(1, -1), slice(0, -2)),
        (slice(1, -1), slice(2, None)),
    ):
        neighbour = values[..., lat_cut, lon_cut]
        face_coef = 0.5 * (middle + coefficients[:, lat_cut, lon_cut])
        updated = updated + face_coef * (neighbour - centre)
    return updated


def clear_outside(values, rim_width, lat_rows):
    lat_pos = (
        lax.axis_index("lat") * lat_rows - rim_width + jnp.arange(values.shape[-2], dtype=jnp.int32)
    )
    inside = (lat_pos >= 0) & (lat_pos < lat_rows * lax.axis_size("lat"))
    return jnp.where(inside[:, None], values, 0.0)


def dynamics(fields, diffusivity):
    kinds, level_rows, lat_rows, lon_cols = fields.shape
    stacked = jnp.concatenate(
        [fields.reshape(kinds * level_rows, lat_rows, lon_cols), diffusivity], axis=0
    )
    stacked = halo_exchange(stacked, STEPS)
    values = stacked[: kinds * level_rows].reshape(
        kinds, level_rows, lat_rows + 2 * STEPS, lon_cols + 2 * STEPS
    )
    kappa = stacked[kinds * level_rows :]
    for repeat in range(STEPS):
        trim = repeat
        coefficients = kappa[:, trim : kappa.shape[1] - trim, trim : kappa.shape[2] - trim]
        values = substep(values, coefficients)
        rim = STEPS - repeat - 1
        if rim:
            values = clear_outside(values, rim, lat_rows)
    return values


def network_kernel(rows_ref, first_ref, middle_hbm, last_ref, out_ref, middle_ref, hidden_ref, sems):
    layers = middle_ref.shape[0]
    copies = [
        pltpu.make_async_copy(middle_hbm.at[layer_no], middle_ref.at[layer_no], sems.at[layer_no])
        for layer_no in range(layers)
    ]
    for copy in copies:
        copy.start()
    hidden_ref[...] = jax.nn.gelu(
        jnp.dot(rows_ref[...], first_ref[...], preferred_element_type=jnp.float32)
    ).astype(jnp.bfloat16)
    for layer_no in range(layers):
        copies[layer_no].wait()
        hidden_ref[...] = jax.nn.gelu(
            jnp.dot(hidden_ref[...], middle_ref[layer_no], preferred_element_type=jnp.float32)
        ).astype(jnp.bfloat16)
    out_ref[...] = jnp.dot(
        hidden_ref[...], last_ref[...], preferred_element_type=jnp.float32
    ).astype(jnp.bfloat16)


def network(rows, w_first, w_middle, w_last):
    count, width = rows.shape
    hid = w_first.shape[1]
    vmem = pl.BlockSpec(memory_space=pltpu.VMEM)
    flops = 2 * count * (width * hid + w_middle.shape[0] * hid * hid + hid * w_last.shape[1])
    weight_bytes = 2 * (w_first.size + w_middle.size + w_last.size)
    return pl.pallas_call(
        network_kernel,
        out_shape=jax.ShapeDtypeStruct((count, w_last.shape[1]), jnp.bfloat16),
        in_specs=[vmem, vmem, pl.BlockSpec(memory_space=pl.ANY), vmem],
        out_specs=vmem,
        scratch_shapes=[
            pltpu.VMEM(w_middle.shape, w_middle.dtype),
            pltpu.VMEM((count, hid), jnp.bfloat16),
            pltpu.SemaphoreType.DMA((w_middle.shape[0],)),
        ],
        compiler_params=pltpu.CompilerParams(vmem_limit_bytes=60 * 1024 * 1024),
        cost_estimate=pl.CostEstimate(
            flops=flops,
            transcendentals=(1 + w_middle.shape[0]) * count * hid,
            bytes_accessed=weight_bytes + 2 * count * (width + w_last.shape[1]),
        ),
    )(rows, w_first, w_middle, w_last)


def on_device(fields, diffusivity, cloudy_index, owners, w_in, w_mid, w_out):
    values = dynamics(fields, diffusivity)
    lev_count = lax.axis_size("lev")
    lon_count = lax.axis_size("lon")
    level_rows = values.shape[1]
    cells = values.shape[2] * values.shape[3]
    column_ids = cloudy_index[0]
    cloudy = column_ids.shape[0]
    per_device = cloudy // lev_count
    capacity = min(per_device, 4 * per_device // lon_count)
    feature_count = 2 * LEVELS
    lat_rows, lon_cols = values.shape[2], values.shape[3]
    local_features = 2 * level_rows
    planes = values.reshape(local_features, lat_rows, lon_cols)
    row_of = column_ids // lon_cols
    col_of = column_ids % lon_cols
    col_picker = (jnp.arange(lon_cols, dtype=jnp.int32)[:, None] == col_of[None, :]).astype(
        jnp.bfloat16
    )
    row_match = jnp.arange(lat_rows, dtype=jnp.int32)[:, None] == row_of[None, :]
    by_row = jnp.dot(
        planes.astype(jnp.bfloat16).reshape(local_features * lat_rows, lon_cols),
        col_picker,
        preferred_element_type=jnp.bfloat16,
    ).reshape(local_features, lat_rows, cloudy)
    picked = jnp.sum(jnp.where(row_match[None], by_row, jnp.zeros_like(by_row)), axis=1)
    routes = owners[0, :, 0]
    group = lon_count * lev_count
    whole_slices = capacity == per_device
    if whole_slices:
        send_buffer = jnp.broadcast_to(
            picked.reshape(local_features, 1, lev_count, per_device),
            (local_features, lon_count, lev_count, per_device),
        ).reshape(local_features, group, capacity)
    else:
        pieces = routes.reshape(lev_count, per_device)
        onehot = (pieces[:, :, None] == jnp.arange(lon_count, dtype=jnp.int32)).astype(jnp.int32)
        slot_rank = jnp.sum(jnp.cumsum(onehot, 1) * onehot, 2) - 1
        piece_of = jnp.arange(lev_count, dtype=jnp.int32)[:, None]
        slot_index = ((pieces * lev_count + piece_of) * capacity + slot_rank).reshape(cloudy)
        send_buffer = (
            jnp.zeros((local_features, group * capacity), jnp.bfloat16)
            .at[:, slot_index]
            .set(picked)
        ).reshape(local_features, group, capacity)
    received = lax.all_to_all(
        send_buffer, ("lon", "lev"), split_axis=1, concat_axis=1, tiled=True
    )
    inputs = (
        received.reshape(2, level_rows, lon_count, lev_count, capacity)
        .transpose(2, 4, 0, 3, 1)
        .reshape(lon_count * capacity, feature_count)
    )
    outcome = network(inputs, w_in[0], w_mid[0], w_out[0])
    outgoing = (
        outcome.reshape(lon_count, capacity, 2, lev_count, level_rows)
        .transpose(2, 4, 0, 3, 1)
        .reshape(local_features, group, capacity)
    )
    returned = lax.all_to_all(
        outgoing, ("lon", "lev"), split_axis=1, concat_axis=1, tiled=True
    )
    if whole_slices:
        returned = returned.reshape(local_features, lon_count, cloudy)
        tendency = returned[:, 0]
        for regime in range(1, lon_count):
            tendency = jnp.where(routes[None, :] == regime, returned[:, regime], tendency)
    else:
        tendency = returned.reshape(local_features, group * capacity)[:, slot_index]
    spread_rows = jnp.where(row_match[None], tendency[:, None, :], jnp.zeros_like(tendency)[:, None, :])
    spread = lax.dot_general(
        spread_rows.reshape(local_features * lat_rows, cloudy),
        col_picker,
        (((1,), (1,)), ((), ())),
        preferred_element_type=jnp.float32,
    )
    updated = planes + spread.reshape(planes.shape)
    return updated.reshape(values.shape)


def solution(mesh):
    in_specs = (
        P(None, "lev", "lat", "lon"),
        P("lev", "lat", "lon"),
        P("lat", "lon"),
        P("lat", "lon", None),
        P("lon", None, None),
        P("lon", None, None, None),
        P("lon", None, None),
    )
    out_specs = P(None, "lev", "lat", "lon")
    return jax.shard_map(
        on_device, mesh=mesh, in_specs=in_specs, out_specs=out_specs, check_vma=False
    )
```

```python
import jax
import jax.numpy as jnp
from jax import lax
from jax.experimental import pallas as pl
from jax.experimental.pallas import tpu as pltpu
from jax.sharding import PartitionSpec as P

LEVELS = 60
STEPS = 3


def halo_exchange(cells, width):
    lat_count = lax.axis_size("lat")
    from_above = lax.ppermute(
        cells[..., cells.shape[-2] - width :, :], "lat", [(i, i + 1) for i in range(lat_count - 1)]
    )
    from_below = lax.ppermute(
        cells[..., :width, :], "lat", [(i + 1, i) for i in range(lat_count - 1)]
    )
    cells = jnp.concatenate([from_above, cells, from_below], axis=-2)
    lon_count = lax.axis_size("lon")
    left = cells[..., :width]
    right = cells[..., cells.shape[-1] - width :]
    if lon_count == 2:
        both = lax.ppermute(jnp.concatenate([right, left], axis=-1), "lon", [(0, 1), (1, 0)])
        from_left, from_right = both[..., :width], both[..., width:]
    else:
        from_left = lax.ppermute(right, "lon", [(i, (i + 1) % lon_count) for i in range(lon_count)])
        from_right = lax.ppermute(left, "lon", [((i + 1) % lon_count, i) for i in range(lon_count)])
    return jnp.concatenate([from_left, cells, from_right], axis=-1)


def substep(values, coefficients):
    centre = values[..., 1:-1, 1:-1]
    middle = coefficients[:, 1:-1, 1:-1]
    updated = centre
    for lat_cut, lon_cut in (
        (slice(0, -2), slice(1, -1)),
        (slice(2, None), slice(1, -1)),
        (slice(1, -1), slice(0, -2)),
        (slice(1, -1), slice(2, None)),
    ):
        neighbour = values[..., lat_cut, lon_cut]
        face_coef = 0.5 * (middle + coefficients[:, lat_cut, lon_cut])
        updated = updated + face_coef * (neighbour - centre)
    return updated


def clear_outside(values, rim_width, lat_rows):
    lat_pos = (
        lax.axis_index("lat") * lat_rows - rim_width + jnp.arange(values.shape[-2], dtype=jnp.int32)
    )
    inside = (lat_pos >= 0) & (lat_pos < lat_rows * lax.axis_size("lat"))
    return jnp.where(inside[:, None], values, 0.0)


def dynamics(fields, diffusivity):
    kinds, level_rows, lat_rows, lon_cols = fields.shape
    stacked = jnp.concatenate(
        [fields.reshape(kinds * level_rows, lat_rows, lon_cols), diffusivity], axis=0
    )
    stacked = halo_exchange(stacked, STEPS)
    values = stacked[: kinds * level_rows].reshape(
        kinds, level_rows, lat_rows + 2 * STEPS, lon_cols + 2 * STEPS
    )
    kappa = stacked[kinds * level_rows :]
    for repeat in range(STEPS):
        trim = repeat
        coefficients = kappa[:, trim : kappa.shape[1] - trim, trim : kappa.shape[2] - trim]
        values = substep(values, coefficients)
        rim = STEPS - repeat - 1
        if rim:
            values = clear_outside(values, rim, lat_rows)
    return values


def network_kernel(rows_ref, first_ref, middle_ref, last_ref, out_ref):
    tile = min(rows_ref.shape[0], 512)

    def one_tile(index, carry):
        rows = pl.ds(pl.multiple_of(index * tile, tile), tile)
        hidden = jax.nn.gelu(
            jnp.dot(rows_ref[rows, :], first_ref[...], preferred_element_type=jnp.float32)
        ).astype(jnp.bfloat16)
        for layer_no in range(middle_ref.shape[0]):
            hidden = jax.nn.gelu(
                jnp.dot(hidden, middle_ref[layer_no], preferred_element_type=jnp.float32)
            ).astype(jnp.bfloat16)
        out_ref[:, rows] = lax.dot_general(
            last_ref[...], hidden, (((1,), (1,)), ((), ())), preferred_element_type=jnp.float32
        ).astype(jnp.bfloat16)
        return carry

    lax.fori_loop(0, rows_ref.shape[0] // tile, one_tile, 0)


def network(rows, w_first, w_middle, w_last):
    count, width = rows.shape
    hid = w_first.shape[1]
    vmem = pl.BlockSpec(memory_space=pltpu.VMEM)
    flops = 2 * count * (width * hid + w_middle.shape[0] * hid * hid + hid * w_last.shape[1])
    weight_bytes = 2 * (w_first.size + w_middle.size + w_last.size)
    return pl.pallas_call(
        network_kernel,
        out_shape=jax.ShapeDtypeStruct((w_last.shape[1], count), jnp.bfloat16),
        in_specs=[vmem] * 4,
        out_specs=vmem,
        compiler_params=pltpu.CompilerParams(vmem_limit_bytes=48 * 1024 * 1024),
        cost_estimate=pl.CostEstimate(
            flops=flops,
            transcendentals=(1 + w_middle.shape[0]) * count * hid,
            bytes_accessed=weight_bytes + 2 * count * (width + w_last.shape[1]),
        ),
    )(rows, w_first, w_middle, w_last.T)


def on_device(fields, diffusivity, cloudy_index, owners, w_in, w_mid, w_out):
    values = dynamics(fields, diffusivity)
    lev_count = lax.axis_size("lev")
    lon_count = lax.axis_size("lon")
    level_rows = values.shape[1]
    cells = values.shape[2] * values.shape[3]
    column_ids = cloudy_index[0]
    cloudy = column_ids.shape[0]
    per_device = cloudy // lev_count
    capacity = min(per_device, 4 * per_device // lon_count)
    feature_count = 2 * LEVELS
    lat_rows, lon_cols = values.shape[2], values.shape[3]
    local_features = 2 * level_rows
    planes = values.reshape(local_features, lat_rows, lon_cols)
    row_of = column_ids // lon_cols
    col_of = column_ids % lon_cols
    col_picker = (jnp.arange(lon_cols, dtype=jnp.int32)[:, None] == col_of[None, :]).astype(
        jnp.bfloat16
    )
    row_match = jnp.arange(lat_rows, dtype=jnp.int32)[:, None] == row_of[None, :]
    by_row = jnp.dot(
        planes.astype(jnp.bfloat16).reshape(local_features * lat_rows, lon_cols),
        col_picker,
        preferred_element_type=jnp.bfloat16,
    ).reshape(local_features, lat_rows, cloudy)
    picked = jnp.sum(jnp.where(row_match[None], by_row, jnp.zeros_like(by_row)), axis=1)
    routes = owners[0, :, 0]
    group = lon_count * lev_count
    whole_slices = capacity == per_device
    if whole_slices:
        send_buffer = jnp.broadcast_to(
            picked.reshape(local_features, 1, lev_count, per_device),
            (local_features, lon_count, lev_count, per_device),
        ).reshape(local_features, group, capacity)
    else:
        pieces = routes.reshape(lev_count, per_device)
        onehot = (pieces[:, :, None] == jnp.arange(lon_count, dtype=jnp.int32)).astype(jnp.int32)
        slot_rank = jnp.sum(jnp.cumsum(onehot, 1) * onehot, 2) - 1
        piece_of = jnp.arange(lev_count, dtype=jnp.int32)[:, None]
        slot_index = ((pieces * lev_count + piece_of) * capacity + slot_rank).reshape(cloudy)
        send_buffer = (
            jnp.zeros((local_features, group * capacity), jnp.bfloat16)
            .at[:, slot_index]
            .set(picked)
        ).reshape(local_features, group, capacity)
    received = lax.all_to_all(
        send_buffer, ("lon", "lev"), split_axis=1, concat_axis=1, tiled=True
    )
    inputs = (
        received.reshape(2, level_rows, lon_count, lev_count, capacity)
        .transpose(2, 4, 0, 3, 1)
        .reshape(lon_count * capacity, feature_count)
    )
    outcome = network(inputs, w_in[0], w_mid[0], w_out[0])
    outgoing = (
        outcome.reshape(2, lev_count, level_rows, lon_count, capacity)
        .transpose(0, 2, 3, 1, 4)
        .reshape(local_features, group, capacity)
    )
    returned = lax.all_to_all(
        outgoing, ("lon", "lev"), split_axis=1, concat_axis=1, tiled=True
    )
    if whole_slices:
        returned = returned.reshape(local_features, lon_count, cloudy)
        tendency = returned[:, 0]
        for regime in range(1, lon_count):
            tendency = jnp.where(routes[None, :] == regime, returned[:, regime], tendency)
    else:
        tendency = returned.reshape(local_features, group * capacity)[:, slot_index]
    spread_rows = jnp.where(row_match[None], tendency[:, None, :], jnp.zeros_like(tendency)[:, None, :])
    spread = lax.dot_general(
        spread_rows.reshape(local_features * lat_rows, cloudy),
        col_picker,
        (((1,), (1,)), ((), ())),
        preferred_element_type=jnp.float32,
    )
    updated = planes + spread.reshape(planes.shape)
    return updated.reshape(values.shape)


def solution(mesh):
    in_specs = (
        P(None, "lev", "lat", "lon"),
        P("lev", "lat", "lon"),
        P("lat", "lon"),
        P("lat", "lon", None),
        P("lon", None, None),
        P("lon", None, None, None),
        P("lon", None, None),
    )
    out_specs = P(None, "lev", "lat", "lon")
    return jax.shard_map(
        on_device, mesh=mesh, in_specs=in_specs, out_specs=out_specs, check_vma=False
    )
```

```python
import jax
import jax.numpy as jnp
from jax import lax
from jax.experimental import pallas as pl
from jax.experimental.pallas import tpu as pltpu
from jax.sharding import PartitionSpec as P

LEVELS = 60
STEPS = 3


def halo_exchange(cells, width):
    lat_count = lax.axis_size("lat")
    from_above = lax.ppermute(
        cells[..., cells.shape[-2] - width :, :], "lat", [(i, i + 1) for i in range(lat_count - 1)]
    )
    from_below = lax.ppermute(
        cells[..., :width, :], "lat", [(i + 1, i) for i in range(lat_count - 1)]
    )
    cells = jnp.concatenate([from_above, cells, from_below], axis=-2)
    lon_count = lax.axis_size("lon")
    left = cells[..., :width]
    right = cells[..., cells.shape[-1] - width :]
    if lon_count == 2:
        both = lax.ppermute(jnp.concatenate([right, left], axis=-1), "lon", [(0, 1), (1, 0)])
        from_left, from_right = both[..., :width], both[..., width:]
    else:
        from_left = lax.ppermute(right, "lon", [(i, (i + 1) % lon_count) for i in range(lon_count)])
        from_right = lax.ppermute(left, "lon", [((i + 1) % lon_count, i) for i in range(lon_count)])
    return jnp.concatenate([from_left, cells, from_right], axis=-1)


def substep(values, coefficients):
    centre = values[..., 1:-1, 1:-1]
    middle = coefficients[:, 1:-1, 1:-1]
    updated = centre
    for lat_cut, lon_cut in (
        (slice(0, -2), slice(1, -1)),
        (slice(2, None), slice(1, -1)),
        (slice(1, -1), slice(0, -2)),
        (slice(1, -1), slice(2, None)),
    ):
        neighbour = values[..., lat_cut, lon_cut]
        face_coef = 0.5 * (middle + coefficients[:, lat_cut, lon_cut])
        updated = updated + face_coef * (neighbour - centre)
    return updated


def clear_outside(values, rim_width, lat_rows):
    lat_pos = (
        lax.axis_index("lat") * lat_rows - rim_width + jnp.arange(values.shape[-2], dtype=jnp.int32)
    )
    inside = (lat_pos >= 0) & (lat_pos < lat_rows * lax.axis_size("lat"))
    return jnp.where(inside[:, None], values, 0.0)


def dynamics(fields, diffusivity):
    kinds, level_rows, lat_rows, lon_cols = fields.shape
    stacked = jnp.concatenate(
        [fields.reshape(kinds * level_rows, lat_rows, lon_cols), diffusivity], axis=0
    )
    stacked = halo_exchange(stacked, STEPS)
    values = stacked[: kinds * level_rows].reshape(
        kinds, level_rows, lat_rows + 2 * STEPS, lon_cols + 2 * STEPS
    )
    kappa = stacked[kinds * level_rows :]
    for repeat in range(STEPS):
        trim = repeat
        coefficients = kappa[:, trim : kappa.shape[1] - trim, trim : kappa.shape[2] - trim]
        values = substep(values, coefficients)
        rim = STEPS - repeat - 1
        if rim:
            values = clear_outside(values, rim, lat_rows)
    return values


def network_kernel(rows_ref, first_ref, middle_ref, last_ref, out_ref):
    tile = min(rows_ref.shape[0], 512)

    def one_tile(index, carry):
        rows = pl.ds(pl.multiple_of(index * tile, tile), tile)
        hidden = jax.nn.gelu(
            jnp.dot(rows_ref[rows, :], first_ref[...], preferred_element_type=jnp.float32)
        ).astype(jnp.bfloat16)
        for layer_no in range(middle_ref.shape[0]):
            hidden = jax.nn.gelu(
                jnp.dot(hidden, middle_ref[layer_no], preferred_element_type=jnp.float32)
            ).astype(jnp.bfloat16)
        out_ref[:, rows] = lax.dot_general(
            last_ref[...], hidden, (((1,), (1,)), ((), ())), preferred_element_type=jnp.float32
        ).astype(jnp.bfloat16)
        return carry

    lax.fori_loop(0, rows_ref.shape[0] // tile, one_tile, 0)


def network(rows, w_first, w_middle, w_last):
    count, width = rows.shape
    hid = w_first.shape[1]
    vmem = pl.BlockSpec(memory_space=pltpu.VMEM)
    flops = 2 * count * (width * hid + w_middle.shape[0] * hid * hid + hid * w_last.shape[1])
    weight_bytes = 2 * (w_first.size + w_middle.size + w_last.size)
    return pl.pallas_call(
        network_kernel,
        out_shape=jax.ShapeDtypeStruct((w_last.shape[1], count), jnp.bfloat16),
        in_specs=[vmem] * 4,
        out_specs=vmem,
        compiler_params=pltpu.CompilerParams(vmem_limit_bytes=48 * 1024 * 1024),
        cost_estimate=pl.CostEstimate(
            flops=flops,
            transcendentals=(1 + w_middle.shape[0]) * count * hid,
            bytes_accessed=weight_bytes + 2 * count * (width + w_last.shape[1]),
        ),
    )(rows, w_first, w_middle, w_last.T)


def on_device(fields, diffusivity, cloudy_index, owners, w_in, w_mid, w_out):
    values = dynamics(fields, diffusivity)
    lev_count = lax.axis_size("lev")
    lon_count = lax.axis_size("lon")
    level_rows = values.shape[1]
    cells = values.shape[2] * values.shape[3]
    column_ids = cloudy_index[0]
    cloudy = column_ids.shape[0]
    per_device = cloudy // lev_count
    capacity = min(per_device, 4 * per_device // lon_count)
    feature_count = 2 * LEVELS
    lat_rows, lon_cols = values.shape[2], values.shape[3]
    local_features = 2 * level_rows
    planes = values.reshape(local_features, lat_rows, lon_cols)
    row_of = column_ids // lon_cols
    col_of = column_ids % lon_cols
    col_picker = (jnp.arange(lon_cols, dtype=jnp.int32)[:, None] == col_of[None, :]).astype(
        jnp.bfloat16
    )
    row_match = jnp.arange(lat_rows, dtype=jnp.int32)[:, None] == row_of[None, :]
    by_row = jnp.dot(
        planes.astype(jnp.bfloat16).reshape(local_features * lat_rows, lon_cols),
        col_picker,
        preferred_element_type=jnp.bfloat16,
    ).reshape(local_features, lat_rows, cloudy)
    picked = jnp.sum(jnp.where(row_match[None], by_row, jnp.zeros_like(by_row)), axis=1)
    routes = owners[0, :, 0]
    group = lon_count * lev_count
    whole_slices = capacity == per_device
    if whole_slices:
        send_buffer = jnp.broadcast_to(
            picked.reshape(local_features, 1, lev_count, per_device),
            (local_features, lon_count, lev_count, per_device),
        ).reshape(local_features, group, capacity)
    else:
        pieces = routes.reshape(lev_count, per_device)
        onehot = (pieces[:, :, None] == jnp.arange(lon_count, dtype=jnp.int32)).astype(jnp.int32)
        slot_rank = jnp.sum(jnp.cumsum(onehot, 1) * onehot, 2) - 1
        piece_of = jnp.arange(lev_count, dtype=jnp.int32)[:, None]
        slot_index = ((pieces * lev_count + piece_of) * capacity + slot_rank).reshape(cloudy)
        send_buffer = (
            jnp.zeros((local_features, group * capacity), jnp.bfloat16)
            .at[:, slot_index]
            .set(picked)
        ).reshape(local_features, group, capacity)
    received = lax.all_to_all(
        send_buffer, ("lon", "lev"), split_axis=1, concat_axis=1, tiled=True
    )
    inputs = (
        received.reshape(2, level_rows, lon_count, lev_count, capacity)
        .transpose(2, 4, 0, 3, 1)
        .reshape(lon_count * capacity, feature_count)
    )
    padded_features = 8 * ((local_features + 7) // 8)
    last_layer = jnp.pad(
        w_out[0]
        .reshape(w_out.shape[1], 2, lev_count, level_rows)
        .transpose(0, 2, 1, 3)
        .reshape(w_out.shape[1], lev_count, local_features),
        ((0, 0), (0, 0), (0, padded_features - local_features)),
    ).reshape(w_out.shape[1], lev_count * padded_features)
    outcome = network(inputs, w_in[0], w_mid[0], last_layer)
    outgoing = (
        outcome.reshape(lev_count, padded_features, lon_count, capacity)
        .transpose(2, 0, 1, 3)
        .reshape(group, padded_features, capacity)
    )
    returned = lax.all_to_all(
        outgoing, ("lon", "lev"), split_axis=0, concat_axis=0, tiled=True
    )[:, :local_features]
    if whole_slices:
        returned = (
            returned.reshape(lon_count, lev_count, local_features, capacity)
            .transpose(0, 2, 1, 3)
            .reshape(lon_count, local_features, cloudy)
        )
        tendency = returned[0]
        for regime in range(1, lon_count):
            tendency = jnp.where(routes[None, :] == regime, returned[regime], tendency)
    else:
        tendency = returned.transpose(1, 0, 2).reshape(local_features, group * capacity)[:, slot_index]
    spread_rows = jnp.where(row_match[None], tendency[:, None, :], jnp.zeros_like(tendency)[:, None, :])
    spread = lax.dot_general(
        spread_rows.reshape(local_features * lat_rows, cloudy),
        col_picker,
        (((1,), (1,)), ((), ())),
        preferred_element_type=jnp.float32,
    )
    updated = planes + spread.reshape(planes.shape)
    return updated.reshape(values.shape)


def solution(mesh):
    in_specs = (
        P(None, "lev", "lat", "lon"),
        P("lev", "lat", "lon"),
        P("lat", "lon"),
        P("lat", "lon", None),
        P("lon", None, None),
        P("lon", None, None, None),
        P("lon", None, None),
    )
    out_specs = P(None, "lev", "lat", "lon")
    return jax.shard_map(
        on_device, mesh=mesh, in_specs=in_specs, out_specs=out_specs, check_vma=False
    )
```

```python
import jax
import jax.numpy as jnp
from jax import lax
from jax.experimental import pallas as pl
from jax.experimental.pallas import tpu as pltpu
from jax.sharding import PartitionSpec as P

LEVELS = 60
STEPS = 3


def halo_exchange(cells, width):
    lat_count = lax.axis_size("lat")
    from_above = lax.ppermute(
        cells[..., cells.shape[-2] - width :, :], "lat", [(i, i + 1) for i in range(lat_count - 1)]
    )
    from_below = lax.ppermute(
        cells[..., :width, :], "lat", [(i + 1, i) for i in range(lat_count - 1)]
    )
    cells = jnp.concatenate([from_above, cells, from_below], axis=-2)
    lon_count = lax.axis_size("lon")
    left = cells[..., :width]
    right = cells[..., cells.shape[-1] - width :]
    if lon_count == 2:
        both = lax.ppermute(jnp.concatenate([right, left], axis=-1), "lon", [(0, 1), (1, 0)])
        from_left, from_right = both[..., :width], both[..., width:]
    else:
        from_left = lax.ppermute(right, "lon", [(i, (i + 1) % lon_count) for i in range(lon_count)])
        from_right = lax.ppermute(left, "lon", [((i + 1) % lon_count, i) for i in range(lon_count)])
    return jnp.concatenate([from_left, cells, from_right], axis=-1)


def substep(values, coefficients):
    centre = values[..., 1:-1, 1:-1]
    middle = coefficients[:, 1:-1, 1:-1]
    updated = centre
    for lat_cut, lon_cut in (
        (slice(0, -2), slice(1, -1)),
        (slice(2, None), slice(1, -1)),
        (slice(1, -1), slice(0, -2)),
        (slice(1, -1), slice(2, None)),
    ):
        neighbour = values[..., lat_cut, lon_cut]
        face_coef = 0.5 * (middle + coefficients[:, lat_cut, lon_cut])
        updated = updated + face_coef * (neighbour - centre)
    return updated


def clear_outside(values, rim_width, lat_rows):
    lat_pos = (
        lax.axis_index("lat") * lat_rows - rim_width + jnp.arange(values.shape[-2], dtype=jnp.int32)
    )
    inside = (lat_pos >= 0) & (lat_pos < lat_rows * lax.axis_size("lat"))
    return jnp.where(inside[:, None], values, 0.0)


def dynamics(fields, diffusivity):
    kinds, level_rows, lat_rows, lon_cols = fields.shape
    stacked = jnp.concatenate(
        [fields.reshape(kinds * level_rows, lat_rows, lon_cols), diffusivity], axis=0
    )
    stacked = halo_exchange(stacked, STEPS)
    values = stacked[: kinds * level_rows].reshape(
        kinds, level_rows, lat_rows + 2 * STEPS, lon_cols + 2 * STEPS
    )
    kappa = stacked[kinds * level_rows :]
    for repeat in range(STEPS):
        trim = repeat
        coefficients = kappa[:, trim : kappa.shape[1] - trim, trim : kappa.shape[2] - trim]
        values = substep(values, coefficients)
        rim = STEPS - repeat - 1
        if rim:
            values = clear_outside(values, rim, lat_rows)
    return values


def network_kernel(rows_ref, first_ref, middle_ref, last_ref, out_ref):
    tile = min(rows_ref.shape[0], 512)

    def one_tile(index, carry):
        rows = pl.ds(pl.multiple_of(index * tile, tile), tile)
        hidden = jax.nn.gelu(
            jnp.dot(rows_ref[rows, :], first_ref[...], preferred_element_type=jnp.float32)
        ).astype(jnp.bfloat16)
        for layer_no in range(middle_ref.shape[0]):
            hidden = jax.nn.gelu(
                jnp.dot(hidden, middle_ref[layer_no], preferred_element_type=jnp.float32)
            ).astype(jnp.bfloat16)
        result = lax.dot_general(
            last_ref[...], hidden, (((1,), (1,)), ((), ())), preferred_element_type=jnp.float32
        ).astype(jnp.bfloat16)
        if len(out_ref.shape) == 2:
            out_ref[:, rows] = result
        else:
            pieces, depth, width = out_ref.shape
            slices = result.shape[0] // depth
            for block in range(tile // width):
                for part in range(slices):
                    out_ref[block * slices + part] = result[
                        part * depth : (part + 1) * depth, block * width : (block + 1) * width
                    ]
        return carry

    lax.fori_loop(0, rows_ref.shape[0] // tile, one_tile, 0)


def network(rows, w_first, w_middle, w_last, blocks=None):
    count, width = rows.shape
    hid = w_first.shape[1]
    vmem = pl.BlockSpec(memory_space=pltpu.VMEM)
    flops = 2 * count * (width * hid + w_middle.shape[0] * hid * hid + hid * w_last.shape[1])
    weight_bytes = 2 * (w_first.size + w_middle.size + w_last.size)
    return pl.pallas_call(
        network_kernel,
        out_shape=jax.ShapeDtypeStruct(blocks or (w_last.shape[1], count), jnp.bfloat16),
        in_specs=[vmem] * 4,
        out_specs=vmem,
        compiler_params=pltpu.CompilerParams(vmem_limit_bytes=48 * 1024 * 1024),
        cost_estimate=pl.CostEstimate(
            flops=flops,
            transcendentals=(1 + w_middle.shape[0]) * count * hid,
            bytes_accessed=weight_bytes + 2 * count * (width + w_last.shape[1]),
        ),
    )(rows, w_first, w_middle, w_last.T)


def on_device(fields, diffusivity, cloudy_index, owners, w_in, w_mid, w_out):
    values = dynamics(fields, diffusivity)
    lev_count = lax.axis_size("lev")
    lon_count = lax.axis_size("lon")
    level_rows = values.shape[1]
    cells = values.shape[2] * values.shape[3]
    column_ids = cloudy_index[0]
    cloudy = column_ids.shape[0]
    per_device = cloudy // lev_count
    capacity = min(per_device, 4 * per_device // lon_count)
    feature_count = 2 * LEVELS
    lat_rows, lon_cols = values.shape[2], values.shape[3]
    local_features = 2 * level_rows
    planes = values.reshape(local_features, lat_rows, lon_cols)
    row_of = column_ids // lon_cols
    col_of = column_ids % lon_cols
    col_picker = (jnp.arange(lon_cols, dtype=jnp.int32)[:, None] == col_of[None, :]).astype(
        jnp.bfloat16
    )
    row_match = jnp.arange(lat_rows, dtype=jnp.int32)[:, None] == row_of[None, :]
    by_row = jnp.dot(
        planes.astype(jnp.bfloat16).reshape(local_features * lat_rows, lon_cols),
        col_picker,
        preferred_element_type=jnp.bfloat16,
    ).reshape(local_features, lat_rows, cloudy)
    picked = jnp.sum(jnp.where(row_match[None], by_row, jnp.zeros_like(by_row)), axis=1)
    routes = owners[0, :, 0]
    group = lon_count * lev_count
    whole_slices = capacity == per_device
    if whole_slices:
        send_buffer = jnp.broadcast_to(
            picked.reshape(local_features, 1, lev_count, per_device),
            (local_features, lon_count, lev_count, per_device),
        ).reshape(local_features, group, capacity)
    else:
        pieces = routes.reshape(lev_count, per_device)
        onehot = (pieces[:, :, None] == jnp.arange(lon_count, dtype=jnp.int32)).astype(jnp.int32)
        slot_rank = jnp.sum(jnp.cumsum(onehot, 1) * onehot, 2) - 1
        piece_of = jnp.arange(lev_count, dtype=jnp.int32)[:, None]
        slot_index = ((pieces * lev_count + piece_of) * capacity + slot_rank).reshape(cloudy)
        send_buffer = (
            jnp.zeros((local_features, group * capacity), jnp.bfloat16)
            .at[:, slot_index]
            .set(picked)
        ).reshape(local_features, group, capacity)
    received = lax.all_to_all(
        send_buffer, ("lon", "lev"), split_axis=1, concat_axis=1, tiled=True
    )
    inputs = (
        received.reshape(2, level_rows, lon_count, lev_count, capacity)
        .transpose(2, 4, 0, 3, 1)
        .reshape(lon_count * capacity, feature_count)
    )
    padded_features = 8 * ((local_features + 7) // 8)
    last_layer = jnp.pad(
        w_out[0]
        .reshape(w_out.shape[1], 2, lev_count, level_rows)
        .transpose(0, 2, 1, 3)
        .reshape(w_out.shape[1], lev_count, local_features),
        ((0, 0), (0, 0), (0, padded_features - local_features)),
    ).reshape(w_out.shape[1], lev_count * padded_features)
    if lon_count * capacity <= 512 and capacity % 128 == 0:
        outgoing = network(
            inputs, w_in[0], w_mid[0], last_layer, (group, padded_features, capacity)
        )
    else:
        outgoing = (
            network(inputs, w_in[0], w_mid[0], last_layer)
            .reshape(lev_count, padded_features, lon_count, capacity)
            .transpose(2, 0, 1, 3)
            .reshape(group, padded_features, capacity)
        )
    returned = lax.all_to_all(
        outgoing, ("lon", "lev"), split_axis=0, concat_axis=0, tiled=True
    )[:, :local_features]
    if whole_slices:
        returned = (
            returned.reshape(lon_count, lev_count, local_features, capacity)
            .transpose(0, 2, 1, 3)
            .reshape(lon_count, local_features, cloudy)
        )
        tendency = returned[0]
        for regime in range(1, lon_count):
            tendency = jnp.where(routes[None, :] == regime, returned[regime], tendency)
    else:
        tendency = returned.transpose(1, 0, 2).reshape(local_features, group * capacity)[:, slot_index]
    spread_rows = jnp.where(row_match[None], tendency[:, None, :], jnp.zeros_like(tendency)[:, None, :])
    spread = lax.dot_general(
        spread_rows.reshape(local_features * lat_rows, cloudy),
        col_picker,
        (((1,), (1,)), ((), ())),
        preferred_element_type=jnp.float32,
    )
    updated = planes + spread.reshape(planes.shape)
    return updated.reshape(values.shape)


def solution(mesh):
    in_specs = (
        P(None, "lev", "lat", "lon"),
        P("lev", "lat", "lon"),
        P("lat", "lon"),
        P("lat", "lon", None),
        P("lon", None, None),
        P("lon", None, None, None),
        P("lon", None, None),
    )
    out_specs = P(None, "lev", "lat", "lon")
    return jax.shard_map(
        on_device, mesh=mesh, in_specs=in_specs, out_specs=out_specs, check_vma=False
    )
```

```python
import jax
import jax.numpy as jnp
from jax import lax
from jax.experimental import pallas as pl
from jax.experimental.pallas import tpu as pltpu
from jax.sharding import PartitionSpec as P

LEVELS = 60
STEPS = 3


def halo_exchange(cells, width):
    lat_count = lax.axis_size("lat")
    from_above = lax.ppermute(
        cells[..., cells.shape[-2] - width :, :], "lat", [(i, i + 1) for i in range(lat_count - 1)]
    )
    from_below = lax.ppermute(
        cells[..., :width, :], "lat", [(i + 1, i) for i in range(lat_count - 1)]
    )
    cells = jnp.concatenate([from_above, cells, from_below], axis=-2)
    lon_count = lax.axis_size("lon")
    left = cells[..., :width]
    right = cells[..., cells.shape[-1] - width :]
    if lon_count == 2:
        both = lax.ppermute(jnp.concatenate([right, left], axis=-1), "lon", [(0, 1), (1, 0)])
        from_left, from_right = both[..., :width], both[..., width:]
    else:
        from_left = lax.ppermute(right, "lon", [(i, (i + 1) % lon_count) for i in range(lon_count)])
        from_right = lax.ppermute(left, "lon", [((i + 1) % lon_count, i) for i in range(lon_count)])
    return jnp.concatenate([from_left, cells, from_right], axis=-1)


def substep(values, coefficients):
    centre = values[..., 1:-1, 1:-1]
    middle = coefficients[:, 1:-1, 1:-1]
    updated = centre
    for lat_cut, lon_cut in (
        (slice(0, -2), slice(1, -1)),
        (slice(2, None), slice(1, -1)),
        (slice(1, -1), slice(0, -2)),
        (slice(1, -1), slice(2, None)),
    ):
        neighbour = values[..., lat_cut, lon_cut]
        face_coef = 0.5 * (middle + coefficients[:, lat_cut, lon_cut])
        updated = updated + face_coef * (neighbour - centre)
    return updated


def clear_outside(values, rim_width, lat_rows):
    lat_pos = (
        lax.axis_index("lat") * lat_rows - rim_width + jnp.arange(values.shape[-2], dtype=jnp.int32)
    )
    inside = (lat_pos >= 0) & (lat_pos < lat_rows * lax.axis_size("lat"))
    return jnp.where(inside[:, None], values, 0.0)


def dynamics(fields, diffusivity):
    kinds, level_rows, lat_rows, lon_cols = fields.shape
    stacked = jnp.concatenate(
        [fields.reshape(kinds * level_rows, lat_rows, lon_cols), diffusivity], axis=0
    )
    stacked = halo_exchange(stacked, STEPS)
    values = stacked[: kinds * level_rows].reshape(
        kinds, level_rows, lat_rows + 2 * STEPS, lon_cols + 2 * STEPS
    )
    kappa = stacked[kinds * level_rows :]
    for repeat in range(STEPS):
        trim = repeat
        coefficients = kappa[:, trim : kappa.shape[1] - trim, trim : kappa.shape[2] - trim]
        values = substep(values, coefficients)
        rim = STEPS - repeat - 1
        if rim:
            values = clear_outside(values, rim, lat_rows)
    return values


def network_kernel(rows_ref, first_ref, middle_ref, last_ref, out_ref):
    tile = min(rows_ref.shape[0], 512)

    def one_tile(index, carry):
        rows = pl.ds(pl.multiple_of(index * tile, tile), tile)
        hidden = jax.nn.gelu(
            jnp.dot(rows_ref[rows, :], first_ref[...], preferred_element_type=jnp.float32)
        ).astype(jnp.bfloat16)
        for layer_no in range(middle_ref.shape[0]):
            hidden = jax.nn.gelu(
                jnp.dot(hidden, middle_ref[layer_no], preferred_element_type=jnp.float32)
            ).astype(jnp.bfloat16)
        out_ref[:, rows] = lax.dot_general(
            last_ref[...], hidden, (((1,), (1,)), ((), ())), preferred_element_type=jnp.float32
        ).astype(jnp.bfloat16)
        return carry

    lax.fori_loop(0, rows_ref.shape[0] // tile, one_tile, 0)


def network(rows, w_first, w_middle, w_last):
    count, width = rows.shape
    hid = w_first.shape[1]
    vmem = pl.BlockSpec(memory_space=pltpu.VMEM)
    flops = 2 * count * (width * hid + w_middle.shape[0] * hid * hid + hid * w_last.shape[1])
    weight_bytes = 2 * (w_first.size + w_middle.size + w_last.size)
    return pl.pallas_call(
        network_kernel,
        out_shape=jax.ShapeDtypeStruct((w_last.shape[1], count), jnp.bfloat16),
        in_specs=[vmem] * 4,
        out_specs=vmem,
        compiler_params=pltpu.CompilerParams(vmem_limit_bytes=48 * 1024 * 1024),
        cost_estimate=pl.CostEstimate(
            flops=flops,
            transcendentals=(1 + w_middle.shape[0]) * count * hid,
            bytes_accessed=weight_bytes + 2 * count * (width + w_last.shape[1]),
        ),
    )(rows, w_first, w_middle, w_last.T)


def on_device(fields, diffusivity, cloudy_index, owners, w_in, w_mid, w_out):
    values = dynamics(fields, diffusivity)
    lev_count = lax.axis_size("lev")
    lon_count = lax.axis_size("lon")
    level_rows = values.shape[1]
    cells = values.shape[2] * values.shape[3]
    column_ids = cloudy_index[0]
    cloudy = column_ids.shape[0]
    per_device = cloudy // lev_count
    capacity = min(per_device, 4 * per_device // lon_count)
    feature_count = 2 * LEVELS
    lat_rows, lon_cols = values.shape[2], values.shape[3]
    local_features = 2 * level_rows
    planes = values.reshape(local_features, lat_rows, lon_cols)
    row_of = column_ids // lon_cols
    col_of = column_ids % lon_cols
    col_picker = (jnp.arange(lon_cols, dtype=jnp.int32)[:, None] == col_of[None, :]).astype(
        jnp.bfloat16
    )
    row_match = jnp.arange(lat_rows, dtype=jnp.int32)[:, None] == row_of[None, :]
    by_row = jnp.dot(
        planes.astype(jnp.bfloat16).reshape(local_features * lat_rows, lon_cols),
        col_picker,
        preferred_element_type=jnp.bfloat16,
    ).reshape(local_features, lat_rows, cloudy)
    picked = jnp.sum(jnp.where(row_match[None], by_row, jnp.zeros_like(by_row)), axis=1)
    routes = owners[0, :, 0]
    group = lon_count * lev_count
    whole_slices = capacity == per_device
    if whole_slices:
        doubled = jnp.dot(
            planes.astype(jnp.bfloat16).reshape(local_features * lat_rows, lon_cols),
            jnp.concatenate([col_picker] * lon_count, axis=1),
            preferred_element_type=jnp.bfloat16,
        ).reshape(local_features, lat_rows, lon_count * cloudy)
        doubled_match = jnp.concatenate([row_match] * lon_count, axis=1)
        send_buffer = jnp.sum(
            jnp.where(doubled_match[None], doubled, jnp.zeros_like(doubled)), axis=1
        ).reshape(local_features, group, capacity)
    else:
        pieces = routes.reshape(lev_count, per_device)
        onehot = (pieces[:, :, None] == jnp.arange(lon_count, dtype=jnp.int32)).astype(jnp.int32)
        slot_rank = jnp.sum(jnp.cumsum(onehot, 1) * onehot, 2) - 1
        piece_of = jnp.arange(lev_count, dtype=jnp.int32)[:, None]
        slot_index = ((pieces * lev_count + piece_of) * capacity + slot_rank).reshape(cloudy)
        send_buffer = (
            jnp.zeros((local_features, group * capacity), jnp.bfloat16)
            .at[:, slot_index]
            .set(picked)
        ).reshape(local_features, group, capacity)
    received = lax.all_to_all(
        send_buffer, ("lon", "lev"), split_axis=1, concat_axis=1, tiled=True
    )
    inputs = (
        received.reshape(2, level_rows, lon_count, lev_count, capacity)
        .transpose(2, 4, 0, 3, 1)
        .reshape(lon_count * capacity, feature_count)
    )
    outcome = network(inputs, w_in[0], w_mid[0], w_out[0])
    outgoing = (
        outcome.reshape(2, lev_count, level_rows, lon_count, capacity)
        .transpose(0, 2, 3, 1, 4)
        .reshape(local_features, group, capacity)
    )
    returned = lax.all_to_all(
        outgoing, ("lon", "lev"), split_axis=1, concat_axis=1, tiled=True
    )
    if whole_slices:
        returned = returned.reshape(local_features, lon_count, cloudy)
        tendency = returned[:, 0]
        for regime in range(1, lon_count):
            tendency = jnp.where(routes[None, :] == regime, returned[:, regime], tendency)
    else:
        tendency = returned.reshape(local_features, group * capacity)[:, slot_index]
    spread_rows = jnp.where(row_match[None], tendency[:, None, :], jnp.zeros_like(tendency)[:, None, :])
    spread = lax.dot_general(
        spread_rows.reshape(local_features * lat_rows, cloudy),
        col_picker,
        (((1,), (1,)), ((), ())),
        preferred_element_type=jnp.float32,
    )
    updated = planes + spread.reshape(planes.shape)
    return updated.reshape(values.shape)


def solution(mesh):
    in_specs = (
        P(None, "lev", "lat", "lon"),
        P("lev", "lat", "lon"),
        P("lat", "lon"),
        P("lat", "lon", None),
        P("lon", None, None),
        P("lon", None, None, None),
        P("lon", None, None),
    )
    out_specs = P(None, "lev", "lat", "lon")
    return jax.shard_map(
        on_device, mesh=mesh, in_specs=in_specs, out_specs=out_specs, check_vma=False
    )
```

```python
import jax
import jax.numpy as jnp
from jax import lax
from jax.experimental import pallas as pl
from jax.experimental.pallas import tpu as pltpu
from jax.sharding import PartitionSpec as P

LEVELS = 60
STEPS = 3


def halo_exchange(cells, width):
    lat_count = lax.axis_size("lat")
    from_above = lax.ppermute(
        cells[..., cells.shape[-2] - width :, :], "lat", [(i, i + 1) for i in range(lat_count - 1)]
    )
    from_below = lax.ppermute(
        cells[..., :width, :], "lat", [(i + 1, i) for i in range(lat_count - 1)]
    )
    cells = jnp.concatenate([from_above, cells, from_below], axis=-2)
    lon_count = lax.axis_size("lon")
    left = cells[..., :width]
    right = cells[..., cells.shape[-1] - width :]
    if lon_count == 2:
        both = lax.ppermute(jnp.concatenate([right, left], axis=-1), "lon", [(0, 1), (1, 0)])
        from_left, from_right = both[..., :width], both[..., width:]
    else:
        from_left = lax.ppermute(right, "lon", [(i, (i + 1) % lon_count) for i in range(lon_count)])
        from_right = lax.ppermute(left, "lon", [((i + 1) % lon_count, i) for i in range(lon_count)])
    return jnp.concatenate([from_left, cells, from_right], axis=-1)


def substep(values, coefficients):
    centre = values[..., 1:-1, 1:-1]
    middle = coefficients[:, 1:-1, 1:-1]
    updated = centre
    for lat_cut, lon_cut in (
        (slice(0, -2), slice(1, -1)),
        (slice(2, None), slice(1, -1)),
        (slice(1, -1), slice(0, -2)),
        (slice(1, -1), slice(2, None)),
    ):
        neighbour = values[..., lat_cut, lon_cut]
        face_coef = 0.5 * (middle + coefficients[:, lat_cut, lon_cut])
        updated = updated + face_coef * (neighbour - centre)
    return updated


def clear_outside(values, rim_width, lat_rows):
    lat_pos = (
        lax.axis_index("lat") * lat_rows - rim_width + jnp.arange(values.shape[-2], dtype=jnp.int32)
    )
    inside = (lat_pos >= 0) & (lat_pos < lat_rows * lax.axis_size("lat"))
    return jnp.where(inside[:, None], values, 0.0)


def dynamics(fields, diffusivity):
    kinds, level_rows, lat_rows, lon_cols = fields.shape
    stacked = jnp.concatenate(
        [fields.reshape(kinds * level_rows, lat_rows, lon_cols), diffusivity], axis=0
    )
    stacked = halo_exchange(stacked, STEPS)
    values = stacked[: kinds * level_rows].reshape(
        kinds, level_rows, lat_rows + 2 * STEPS, lon_cols + 2 * STEPS
    )
    kappa = stacked[kinds * level_rows :]
    for repeat in range(STEPS):
        trim = repeat
        coefficients = kappa[:, trim : kappa.shape[1] - trim, trim : kappa.shape[2] - trim]
        values = substep(values, coefficients)
        rim = STEPS - repeat - 1
        if rim:
            values = clear_outside(values, rim, lat_rows)
    return values


def network_kernel(rows_ref, first_ref, middle_ref, last_ref, out_ref):
    tile = min(rows_ref.shape[1], 512)

    def one_tile(index, carry):
        rows = pl.ds(pl.multiple_of(index * tile, tile), tile)
        hidden = jax.nn.gelu(
            lax.dot_general(
                rows_ref[:, rows], first_ref[...], (((0,), (0,)), ((), ())),
                preferred_element_type=jnp.float32,
            )
        ).astype(jnp.bfloat16)
        for layer_no in range(middle_ref.shape[0]):
            hidden = jax.nn.gelu(
                jnp.dot(hidden, middle_ref[layer_no], preferred_element_type=jnp.float32)
            ).astype(jnp.bfloat16)
        out_ref[:, rows] = lax.dot_general(
            last_ref[...], hidden, (((1,), (1,)), ((), ())), preferred_element_type=jnp.float32
        ).astype(jnp.bfloat16)
        return carry

    lax.fori_loop(0, rows_ref.shape[1] // tile, one_tile, 0)


def network(rows, w_first, w_middle, w_last):
    width, count = rows.shape
    hid = w_first.shape[1]
    vmem = pl.BlockSpec(memory_space=pltpu.VMEM)
    flops = 2 * count * (width * hid + w_middle.shape[0] * hid * hid + hid * w_last.shape[1])
    weight_bytes = 2 * (w_first.size + w_middle.size + w_last.size)
    return pl.pallas_call(
        network_kernel,
        out_shape=jax.ShapeDtypeStruct((w_last.shape[1], count), jnp.bfloat16),
        in_specs=[vmem] * 4,
        out_specs=vmem,
        compiler_params=pltpu.CompilerParams(vmem_limit_bytes=48 * 1024 * 1024),
        cost_estimate=pl.CostEstimate(
            flops=flops,
            transcendentals=(1 + w_middle.shape[0]) * count * hid,
            bytes_accessed=weight_bytes + 2 * count * (width + w_last.shape[1]),
        ),
    )(rows, w_first, w_middle, w_last.T)


def on_device(fields, diffusivity, cloudy_index, owners, w_in, w_mid, w_out):
    values = dynamics(fields, diffusivity)
    lev_count = lax.axis_size("lev")
    lon_count = lax.axis_size("lon")
    level_rows = values.shape[1]
    cells = values.shape[2] * values.shape[3]
    column_ids = cloudy_index[0]
    cloudy = column_ids.shape[0]
    per_device = cloudy // lev_count
    capacity = min(per_device, 4 * per_device // lon_count)
    feature_count = 2 * LEVELS
    lat_rows, lon_cols = values.shape[2], values.shape[3]
    local_features = 2 * level_rows
    planes = values.reshape(local_features, lat_rows, lon_cols)
    row_of = column_ids // lon_cols
    col_of = column_ids % lon_cols
    col_picker = (jnp.arange(lon_cols, dtype=jnp.int32)[:, None] == col_of[None, :]).astype(
        jnp.bfloat16
    )
    row_match = jnp.arange(lat_rows, dtype=jnp.int32)[:, None] == row_of[None, :]
    by_row = jnp.dot(
        planes.astype(jnp.bfloat16).reshape(local_features * lat_rows, lon_cols),
        col_picker,
        preferred_element_type=jnp.bfloat16,
    ).reshape(local_features, lat_rows, cloudy)
    picked = jnp.sum(jnp.where(row_match[None], by_row, jnp.zeros_like(by_row)), axis=1)
    routes = owners[0, :, 0]
    group = lon_count * lev_count
    whole_slices = capacity == per_device
    if whole_slices:
        doubled = jnp.dot(
            planes.astype(jnp.bfloat16).reshape(local_features * lat_rows, lon_cols),
            jnp.concatenate([col_picker] * lon_count, axis=1),
            preferred_element_type=jnp.bfloat16,
        ).reshape(local_features, lat_rows, lon_count * cloudy)
        doubled_match = jnp.concatenate([row_match] * lon_count, axis=1)
        send_buffer = jnp.sum(
            jnp.where(doubled_match[None], doubled, jnp.zeros_like(doubled)), axis=1
        ).reshape(local_features, group, capacity)
    else:
        pieces = routes.reshape(lev_count, per_device)
        onehot = (pieces[:, :, None] == jnp.arange(lon_count, dtype=jnp.int32)).astype(jnp.int32)
        slot_rank = jnp.sum(jnp.cumsum(onehot, 1) * onehot, 2) - 1
        piece_of = jnp.arange(lev_count, dtype=jnp.int32)[:, None]
        slot_index = ((pieces * lev_count + piece_of) * capacity + slot_rank).reshape(cloudy)
        send_buffer = (
            jnp.zeros((local_features, group * capacity), jnp.bfloat16)
            .at[:, slot_index]
            .set(picked)
        ).reshape(local_features, group, capacity)
    received = lax.all_to_all(
        send_buffer, ("lon", "lev"), split_axis=1, concat_axis=1, tiled=True
    )
    inputs = (
        received.reshape(local_features, lon_count, lev_count, capacity)
        .transpose(2, 0, 1, 3)
        .reshape(feature_count, lon_count * capacity)
    )
    first_layer = (
        w_in[0]
        .reshape(2, lev_count, level_rows, w_in.shape[2])
        .transpose(1, 0, 2, 3)
        .reshape(feature_count, w_in.shape[2])
    )
    outcome = network(inputs, first_layer, w_mid[0], w_out[0])
    outgoing = (
        outcome.reshape(2, lev_count, level_rows, lon_count, capacity)
        .transpose(0, 2, 3, 1, 4)
        .reshape(local_features, group, capacity)
    )
    returned = lax.all_to_all(
        outgoing, ("lon", "lev"), split_axis=1, concat_axis=1, tiled=True
    )
    if whole_slices:
        returned = returned.reshape(local_features, lon_count, cloudy)
        tendency = returned[:, 0]
        for regime in range(1, lon_count):
            tendency = jnp.where(routes[None, :] == regime, returned[:, regime], tendency)
    else:
        tendency = returned.reshape(local_features, group * capacity)[:, slot_index]
    spread_rows = jnp.where(row_match[None], tendency[:, None, :], jnp.zeros_like(tendency)[:, None, :])
    spread = lax.dot_general(
        spread_rows.reshape(local_features * lat_rows, cloudy),
        col_picker,
        (((1,), (1,)), ((), ())),
        preferred_element_type=jnp.float32,
    )
    updated = planes + spread.reshape(planes.shape)
    return updated.reshape(values.shape)


def solution(mesh):
    in_specs = (
        P(None, "lev", "lat", "lon"),
        P("lev", "lat", "lon"),
        P("lat", "lon"),
        P("lat", "lon", None),
        P("lon", None, None),
        P("lon", None, None, None),
        P("lon", None, None),
    )
    out_specs = P(None, "lev", "lat", "lon")
    return jax.shard_map(
        on_device, mesh=mesh, in_specs=in_specs, out_specs=out_specs, check_vma=False
    )
```
